512 devices in a mesh: gx: 8 (over x, core), gy: 8 (over y), gz: 8 (over z).
Axes of the slice: x: 4, y: 8, z: 8, core: 2. Of those that a mesh axis runs over, the one named last changes fastest.
Arguments:
- features: bfloat16 [32, 16, 128, 1024], P(None, 'gx', 'gy', 'gz'), may hold values from -6 to 6
- voxel_slot: int32 [16, 128, 1024], P('gx', 'gy', 'gz'), may hold values from 0 to 1023
- conv_weight: bfloat16 [27, 32, 32], replicated, may hold values from -0.21875 to 0.21875
- conv_bias: float32 [32], replicated, may hold values from -3 to 3
- pair_owner: int32 [65536, 1], P(('gx', 'gy', 'gz')), may hold values from 0 to 63; in each aligned block of 128 rows (0 to 127, 128 to 255, ...) at most 5 rows name the same one
- pair_edge: int32 [65536], P(('gx', 'gy', 'gz')), may hold values from 0 to 63
- mlp_in: bfloat16 [256, 512], replicated, may hold values from -0.375 to 0.375
- mlp_in_bias: float32 [512], replicated, may hold values from -3 to 3
- mlp_mid: bfloat16 [512, 512], replicated, may hold values from -0.25 to 0.25
- mlp_mid_bias: float32 [512], replicated, may hold values from -3 to 3
- mlp_out: bfloat16 [512], replicated, may hold values from -0.25 to 0.25
Outputs:
- pair_scores: float32 [65536], P(('gx', 'gy', 'gz'))
The draws below stay inside these ranges and needn't reach their ends.
Inputs may be any that keep to these rules, and one draw needn't show every extreme that they name: `pair_owner`: within each aligned block of 128 rows (the pairs of one brick) no owner is named by more than 5 rows, a bound that some block reaches.
All inputs are finite; a program needn't handle non-finite values.
Results may differ from the reference program's by a relative error of at most 0.011.
Values may be sent and summed in bfloat16 or wider, within the bound.
No kernel may reach another device: no remote copies, remote signals or barrier semaphores. Data moves between devices by JAX's collectives and lax.ppermute only.
A program may use at most 64 MiB of HBM per device.

```python
import math
import jax
import jax.numpy as jnp
import numpy as np
from jax import lax

C = 32
BINS = 8
HID = 512
BX = 2
BY = 16
BZ = 128
P_DEV = 128
EDGE_DEV = 64
ROW = 256
SLOTS = 1024
CAP = 5
NX = 16
NY = 128
NZ = 1024
NPAIRS = 65536
N_GX = 8
N_GY = 8
N_GZ = 8


def place_ends(array, rng, smallest, top_value):
    index_at = [jax.random.randint(jax.random.fold_in(rng, axis), (), 0, length) for axis, length in enumerate(array.shape)]
    main_axis = array.shape.index(max(array.shape))
    beside = index_at[:main_axis] + [(index_at[main_axis] + 1) % array.shape[main_axis]] + index_at[main_axis + 1:]
    return array.at[tuple(index_at)].set(smallest).at[tuple(beside)].set(top_value)


def block_levels(stream_key, dims, shards, low, top_value):
    def one(position, parts):
        heights = jax.random.uniform(jax.random.fold_in(jax.random.fold_in(stream_key, 6), position), (parts,), jnp.float32, low / len(shards), top_value / len(shards))
        return jnp.repeat(jnp.exp(heights), dims[position] // parts).reshape((-1,) + (1,) * (len(dims) - position - 1))

    gain = one(*shards[0])
    for cut in shards[1:]:
        gain = gain * one(*cut)
    return gain


def routed_block(rng, own, number, rows, number_of, top, most, skew):
    sequence = jax.random.permutation(rng, number_of)
    crowded, usual = load_shares(number_of, rows * top, most, skew, True), load_shares(number_of, rows * top, most, skew, False)
    places = jnp.arange(number_of)

    def named(sizes, offset_by):
        used = int((sizes > 0).sum())
        fixed = max(1, used // 4)
        moved = fixed + (places - fixed + offset_by * (used - fixed)) % max(1, number_of - fixed)
        return jnp.zeros((number_of,), jnp.int32).at[sequence[jnp.where(places < fixed, places, moved)]].set(jnp.asarray(sizes, jnp.int32))

    sizes = jnp.where(number % 4 == 0, named(crowded, number // 4), named(usual, number - number // 4 - 1))
    mixed = jax.random.permutation(jax.random.fold_in(own, 3), number_of)
    giver, taker = mixed[0:number_of // 2 * 2:2], mixed[1:number_of // 2 * 2:2]
    room = jnp.minimum(sizes[giver] - 1, most - sizes[taker]) // 2
    room = jnp.where((giver == sequence[0]) | (taker == sequence[0]) | (sizes[taker] == 0), 0, jnp.maximum(room, 0))
    moved = jax.random.randint(jax.random.fold_in(own, 4), (number_of // 2,), 0, 1 << 20) % (room + 1)
    sizes = sizes.at[giver].add(-moved).at[taker].add(moved)
    items = jnp.searchsorted(jnp.cumsum(sizes), jnp.arange(rows * top), side="right").astype(jnp.int32)
    grid = items.reshape(top, rows).T
    grid = grid[jax.random.permutation(jax.random.fold_in(own, 1), rows)]
    offset_by = jax.random.randint(jax.random.fold_in(own, 2), (rows, 1), 0, top)
    return jnp.take_along_axis(grid, (jnp.arange(top)[None, :] + offset_by) % top, axis=1)


def load_shares(number_of, total, bound, lean, full):
    weights = [(1 << 20) // math.isqrt(standing ** lean) + 1 for standing in range(1, number_of + 1)]
    largest = bound if full else min(bound, max(-(-total // number_of), total * weights[0] // sum(weights)))
    least = 1 if total - largest >= number_of - 1 else 0
    holding, spare = [largest] + [least] * (number_of - 1), total - largest - least * (number_of - 1)
    while spare > 0:
        free = [i for i in range(1, number_of) if holding[i] < largest] or [i for i in range(1, number_of) if holding[i] < bound]
        pool, budget = sum([weights[i] for i in free]), spare
        for i in free:
            more = min(bound - holding[i], max(1, budget * weights[i] // pool), spare)
            holding[i] = holding[i] + more
            spare = spare - more
    return np.array(holding)


def centred(rng, dims, deviation, most, shards=(), kind=jnp.bfloat16):
    gain = block_levels(rng, dims, shards, -0.22, 0.18) if shards else 1.0
    result = jax.random.normal(rng, dims, jnp.float32) * deviation * gain
    return jnp.minimum(jnp.maximum(result, -most), most).astype(kind)


def setup_inputs(seed: int = 0) -> dict:
    streams_of = jax.random.split(jax.random.key(seed), 12)
    features = centred(streams_of[0], (C, NX, NY, NZ), 1.0, 6.0, ((1, 8), (2, 8), (3, 8)))
    voxel_slot = place_ends(jax.random.randint(streams_of[1], (NX, NY, NZ), 0, SLOTS), jax.random.fold_in(streams_of[1], 1), 0, SLOTS - 1).astype(jnp.int32)
    conv_weight = centred(streams_of[2], (27, C, C), (27 * C) ** -0.5, 0.21875)
    conv_bias = centred(streams_of[3], (C,), 0.5, 3.0, (), jnp.float32)
    pair_owner_keys = jax.random.split(jax.random.fold_in(streams_of[4], 1), NPAIRS // P_DEV)
    pair_owner_turns = jax.random.permutation(jax.random.fold_in(streams_of[4], 3), NPAIRS // P_DEV)
    pair_owner = jax.vmap(lambda own, number: routed_block(jax.random.fold_in(streams_of[4], 2), own, number, P_DEV, N_GX * N_GY, 1, CAP, 2))(pair_owner_keys, pair_owner_turns).reshape((NPAIRS, 1))
    pair_edge = place_ends(jax.random.randint(streams_of[5], (NPAIRS,), 0, EDGE_DEV), jax.random.fold_in(streams_of[5], 1), 0, EDGE_DEV - 1).astype(jnp.int32)
    mlp_in = centred(streams_of[6], (ROW, HID), ROW ** -0.5, 0.375)
    mlp_in_bias = centred(streams_of[7], (HID,), 0.5, 3.0, (), jnp.float32)
    mlp_mid = centred(streams_of[8], (HID, HID), HID ** -0.5, 0.25)
    mlp_mid_bias = centred(streams_of[9], (HID,), 0.5, 3.0, (), jnp.float32)
    mlp_out = centred(streams_of[10], (HID,), HID ** -0.5, 0.25)
    return {"features": features, "voxel_slot": voxel_slot, "conv_weight": conv_weight, "conv_bias": conv_bias, "pair_owner": pair_owner, "pair_edge": pair_edge, "mlp_in": mlp_in, "mlp_in_bias": mlp_in_bias, "mlp_mid": mlp_mid, "mlp_mid_bias": mlp_mid_bias, "mlp_out": mlp_out}


def reference(features, voxel_slot, conv_weight, conv_bias, pair_owner, pair_edge, mlp_in, mlp_in_bias, mlp_mid, mlp_mid_bias, mlp_out):
    volume_in = features.astype(jnp.float32)[None]
    kernel = conv_weight.astype(jnp.float32).reshape(3, 3, 3, C, C).transpose(3, 4, 0, 1, 2)
    conv_out = lax.conv_general_dilated(volume_in, kernel, (1, 1, 1), "SAME", precision=lax.Precision.HIGHEST)[0]
    fields = jnp.maximum(conv_out + conv_bias[:, None, None, None], 0.0).astype(jnp.bfloat16)
    bricks = N_GX * N_GY * N_GZ
    voxels = BX * BY * BZ
    brick_fields = fields.reshape(C, N_GX, BX, N_GY, BY, N_GZ, BZ).transpose(1, 3, 5, 2, 4, 6, 0).reshape(bricks * voxels, C)
    brick_slots = voxel_slot.reshape(N_GX, BX, N_GY, BY, N_GZ, BZ).transpose(0, 2, 4, 1, 3, 5).reshape(bricks, voxels)
    segment_ids = (brick_slots + (jnp.arange(bricks, dtype=jnp.int32) * SLOTS)[:, None]).reshape(-1)
    pooled = jax.ops.segment_sum(brick_fields.astype(jnp.float32), segment_ids, num_segments=bricks * SLOTS)
    pooled = pooled * (SLOTS / voxels)
    pair_rows = pooled.reshape(bricks, BINS, P_DEV, C).transpose(0, 2, 1, 3).reshape(NPAIRS, ROW).astype(jnp.bfloat16)
    brick_of_pair = jnp.arange(NPAIRS, dtype=jnp.int32) // P_DEV
    plane = brick_of_pair % N_GZ
    edge_ids = ((plane * (N_GX * N_GY) + pair_owner[:, 0]) * EDGE_DEV + pair_edge).astype(jnp.int32)
    edge_total = N_GZ * N_GX * N_GY * EDGE_DEV
    edge_rows = jax.ops.segment_sum(pair_rows.astype(jnp.float32), edge_ids, num_segments=edge_total).astype(jnp.bfloat16)
    first = jax.nn.silu(jnp.dot(edge_rows, mlp_in, preferred_element_type=jnp.float32) + mlp_in_bias).astype(jnp.bfloat16)
    second = jax.nn.silu(jnp.dot(first, mlp_mid, preferred_element_type=jnp.float32) + mlp_mid_bias).astype(jnp.bfloat16)
    edge_scores = jnp.dot(second, mlp_out, preferred_element_type=jnp.float32)
    return edge_scores[edge_ids]
```

```python
import jax
import jax.numpy as jnp
from jax import lax
from jax.sharding import PartitionSpec as P

BINS = 8
EDGE_DEV = 64


def extended(cells, sides, width):
    for axis, dim in sides:
        count = lax.axis_size(axis)
        ends = count - 1
        head = lax.slice_in_dim(cells, 0, width, axis=dim)
        tail = lax.slice_in_dim(cells, cells.shape[dim] - width, cells.shape[dim], axis=dim)
        cells = jnp.concatenate(
            [
                lax.ppermute(tail, axis, [(i, (i + 1) % count) for i in range(ends)]),
                cells,
                lax.ppermute(head, axis, [((i + 1) % count, i) for i in range(ends)]),
            ],
            axis=dim,
        )
    return cells


def body(
    features,
    voxel_slot,
    conv_weight,
    conv_bias,
    pair_owner,
    pair_edge,
    mlp_in,
    mlp_in_bias,
    mlp_mid,
    mlp_mid_bias,
    mlp_out,
):
    channels, extent_x, extent_y, extent_z = features.shape
    volume = extent_x * extent_y * extent_z
    padded = extended(features, (("gx", 1), ("gy", 2), ("gz", 3)), 1)
    kernel = conv_weight.reshape(3, 3, 3, channels, channels).transpose(3, 4, 0, 1, 2)
    total = lax.conv_general_dilated(
        padded[None],
        kernel,
        (1, 1, 1),
        "VALID",
        dimension_numbers=("NCDHW", "OIDHW", "NCDHW"),
        preferred_element_type=jnp.float32,
    )[0].reshape(channels, volume)
    fields = jnp.maximum(total + conv_bias[:, None], 0.0).astype(jnp.bfloat16)
    pair_count = pair_edge.shape[0]
    slot_count = pair_count * BINS
    slots_flat = voxel_slot.reshape(volume)
    block_width = 512
    pieces = []
    for block in range(slot_count // block_width):
        labels = block * block_width + lax.iota(jnp.int32, block_width)
        onehot = (slots_flat[:, None] == labels[None, :]).astype(jnp.bfloat16)
        pieces.append(jnp.dot(fields, onehot, preferred_element_type=jnp.float32))
    pooled = jnp.concatenate(pieces, axis=1) * (slot_count / volume)
    row_width = BINS * channels
    pair_rows = (
        pooled.reshape(channels, BINS, pair_count)
        .transpose(2, 1, 0)
        .reshape(pair_count, row_width)
        .astype(jnp.bfloat16)
    )
    size_gx = lax.axis_size("gx")
    size_gy = lax.axis_size("gy")
    groups = size_gx * size_gy
    capacity = max(2, (5 * pair_count + 2 * groups - 1) // (2 * groups))
    owners = pair_owner[:, 0]
    owner_marks = (owners[:, None] == lax.iota(jnp.int32, groups)[None, :]).astype(jnp.int32)
    earlier = jnp.cumsum(owner_marks, axis=0) - owner_marks
    slot_rank = jnp.sum(earlier * owner_marks, axis=1)
    target = owners * capacity + slot_rank
    send_rows = jnp.zeros((groups * capacity, row_width), jnp.bfloat16).at[target].set(pair_rows)
    send_ids = jnp.full((groups * capacity,), -1, jnp.bfloat16).at[target].set(
        pair_edge.astype(jnp.bfloat16)
    )
    id_row = jnp.pad(send_ids.reshape(groups, 1, capacity), ((0, 0), (0, 0), (0, row_width - capacity)))
    send = jnp.concatenate([send_rows.reshape(groups, capacity, row_width), id_row], axis=1)
    edge_count = EDGE_DEV
    recv = lax.all_to_all(send, ("gx", "gy"), split_axis=0, concat_axis=0, tiled=True)
    flat_rows = recv[:, :capacity, :].reshape(groups * capacity, row_width)
    flat_ids = recv[:, capacity, :capacity].reshape(groups * capacity).astype(jnp.int32)
    edge_onehot = (lax.iota(jnp.int32, edge_count)[:, None] == flat_ids[None, :]).astype(
        jnp.bfloat16
    )
    edge_rows = jnp.dot(edge_onehot, flat_rows, preferred_element_type=jnp.float32).astype(
        jnp.bfloat16
    )
    first = jax.nn.silu(
        jnp.dot(edge_rows, mlp_in, preferred_element_type=jnp.float32) + mlp_in_bias
    ).astype(jnp.bfloat16)
    second = jax.nn.silu(
        jnp.dot(first, mlp_mid, preferred_element_type=jnp.float32) + mlp_mid_bias
    ).astype(jnp.bfloat16)
    edge_scores = jnp.dot(second, mlp_out, preferred_element_type=jnp.float32)
    plane_scores = lax.all_gather(edge_scores.reshape(1, edge_count), ("gx", "gy"), axis=0, tiled=True).reshape(groups * edge_count)
    wanted = owners * edge_count + pair_edge
    picks = wanted[:, None] == lax.iota(jnp.int32, groups * edge_count)[None, :]
    return jnp.sum(jnp.where(picks, plane_scores[None, :], 0.0), axis=1)


def solution(mesh):
    placed = (
        P(None, "gx", "gy", "gz"),
        P("gx", "gy", "gz"),
        P(),
        P(),
        P(("gx", "gy", "gz"), None),
        P(("gx", "gy", "gz")),
        P(),
        P(),
        P(),
        P(),
        P(),
    )
    return jax.shard_map(
        body, mesh=mesh, in_specs=placed, out_specs=P(("gx", "gy", "gz")), check_vma=False
    )
```

```python
import jax
import jax.numpy as jnp
from jax import lax
from jax.sharding import PartitionSpec as P

BINS = 8
EDGE_DEV = 64


def extended(cells, sides, width):
    for axis, dim in sides:
        count = lax.axis_size(axis)
        ends = count - 1
        head = lax.slice_in_dim(cells, 0, width, axis=dim)
        tail = lax.slice_in_dim(cells, cells.shape[dim] - width, cells.shape[dim], axis=dim)
        cells = jnp.concatenate(
            [
                lax.ppermute(tail, axis, [(i, (i + 1) % count) for i in range(ends)]),
                cells,
                lax.ppermute(head, axis, [((i + 1) % count, i) for i in range(ends)]),
            ],
            axis=dim,
        )
    return cells


def body(
    features,
    voxel_slot,
    conv_weight,
    conv_bias,
    pair_owner,
    pair_edge,
    mlp_in,
    mlp_in_bias,
    mlp_mid,
    mlp_mid_bias,
    mlp_out,
):
    channels, extent_x, extent_y, extent_z = features.shape
    volume = extent_x * extent_y * extent_z
    padded = extended(features, (("gx", 1), ("gy", 2), ("gz", 3)), 1)
    kernel = conv_weight.reshape(3, 3, 3, channels, channels).transpose(3, 4, 0, 1, 2)
    total = lax.conv_general_dilated(
        padded[None],
        kernel,
        (1, 1, 1),
        "VALID",
        dimension_numbers=("NCDHW", "OIDHW", "NCDHW"),
        preferred_element_type=jnp.float32,
    )[0].reshape(channels, volume)
    fields = jnp.maximum(total + conv_bias[:, None], 0.0).astype(jnp.bfloat16)
    pair_count = pair_edge.shape[0]
    slot_count = pair_count * BINS
    slots_flat = voxel_slot.reshape(volume)
    block_width = 512
    pieces = []
    for block in range(slot_count // block_width):
        labels = block * block_width + lax.iota(jnp.int32, block_width)
        onehot = (slots_flat[:, None] == labels[None, :]).astype(jnp.bfloat16)
        pieces.append(jnp.dot(fields, onehot, preferred_element_type=jnp.float32))
    pooled = jnp.concatenate(pieces, axis=1) * (slot_count / volume)
    row_width = BINS * channels
    pair_rows = (
        pooled.reshape(channels, BINS, pair_count)
        .transpose(2, 1, 0)
        .reshape(pair_count, row_width)
        .astype(jnp.bfloat16)
    )
    size_gx = lax.axis_size("gx")
    size_gy = lax.axis_size("gy")
    groups = size_gx * size_gy
    capacity = max(2, (5 * pair_count + 2 * groups - 1) // (2 * groups))
    owners = pair_owner[:, 0]
    owner_marks = (owners[:, None] == lax.iota(jnp.int32, groups)[None, :]).astype(jnp.int32)
    earlier = jnp.cumsum(owner_marks, axis=0) - owner_marks
    slot_rank = jnp.sum(earlier * owner_marks, axis=1)
    target = owners * capacity + slot_rank
    send_rows = jnp.zeros((groups * capacity, row_width), jnp.bfloat16).at[target].set(pair_rows)
    send_ids = jnp.full((groups * capacity,), -1, jnp.bfloat16).at[target].set(
        pair_edge.astype(jnp.bfloat16)
    )
    id_row = jnp.pad(send_ids.reshape(groups, 1, capacity), ((0, 0), (0, 0), (0, row_width - capacity)))
    send = jnp.concatenate([send_rows.reshape(groups, capacity, row_width), id_row], axis=1)
    edge_count = EDGE_DEV
    recv = lax.all_to_all(send, ("gx", "gy"), split_axis=0, concat_axis=0, tiled=True)
    flat_rows = recv[:, :capacity, :].reshape(groups * capacity, row_width)
    flat_ids = recv[:, capacity, :capacity].reshape(groups * capacity).astype(jnp.int32)
    edge_onehot = (lax.iota(jnp.int32, edge_count)[:, None] == flat_ids[None, :]).astype(
        jnp.bfloat16
    )
    edge_rows = jnp.dot(edge_onehot, flat_rows, preferred_element_type=jnp.float32).astype(
        jnp.bfloat16
    )
    first = jax.nn.silu(
        jnp.dot(edge_rows, mlp_in, preferred_element_type=jnp.float32) + mlp_in_bias
    ).astype(jnp.bfloat16)
    second = jax.nn.silu(
        jnp.dot(first, mlp_mid, preferred_element_type=jnp.float32) + mlp_mid_bias
    ).astype(jnp.bfloat16)
    edge_scores = jnp.dot(second, mlp_out, preferred_element_type=jnp.float32)
    owner_picks = flat_ids[:, None] == lax.iota(jnp.int32, edge_count)[None, :]
    owner_scores = jnp.sum(jnp.where(owner_picks, edge_scores[None, :], 0.0), axis=1)
    returned = lax.all_to_all(
        owner_scores.reshape(groups, capacity), ("gx", "gy"), split_axis=0, concat_axis=0, tiled=True
    ).reshape(groups * capacity)
    back_picks = target[:, None] == lax.iota(jnp.int32, groups * capacity)[None, :]
    return jnp.sum(jnp.where(back_picks, returned[None, :], 0.0), axis=1)


def solution(mesh):
    placed = (
        P(None, "gx", "gy", "gz"),
        P("gx", "gy", "gz"),
        P(),
        P(),
        P(("gx", "gy", "gz"), None),
        P(("gx", "gy", "gz")),
        P(),
        P(),
        P(),
        P(),
        P(),
    )
    return jax.shard_map(
        body, mesh=mesh, in_specs=placed, out_specs=P(("gx", "gy", "gz")), check_vma=False
    )
```

```python
import jax
import jax.numpy as jnp
from jax import lax
from jax.sharding import PartitionSpec as P

BINS = 8
EDGE_DEV = 64


def extended(cells, sides, width):
    for axis, dim in sides:
        count = lax.axis_size(axis)
        ends = count - 1
        head = lax.slice_in_dim(cells, 0, width, axis=dim)
        tail = lax.slice_in_dim(cells, cells.shape[dim] - width, cells.shape[dim], axis=dim)
        cells = jnp.concatenate(
            [
                lax.ppermute(tail, axis, [(i, (i + 1) % count) for i in range(ends)]),
                cells,
                lax.ppermute(head, axis, [((i + 1) % count, i) for i in range(ends)]),
            ],
            axis=dim,
        )
    return cells


def body(
    features,
    voxel_slot,
    conv_weight,
    conv_bias,
    pair_owner,
    pair_edge,
    mlp_in,
    mlp_in_bias,
    mlp_mid,
    mlp_mid_bias,
    mlp_out,
):
    channels, extent_x, extent_y, extent_z = features.shape
    volume = extent_x * extent_y * extent_z
    padded = extended(features, (("gx", 1), ("gy", 2), ("gz", 3)), 1)
    kernel = conv_weight.reshape(3, 3, 3, channels, channels).transpose(3, 4, 0, 1, 2)
    total = lax.conv_general_dilated(
        padded[None],
        kernel,
        (1, 1, 1),
        "VALID",
        dimension_numbers=("NCDHW", "OIDHW", "NCDHW"),
        preferred_element_type=jnp.float32,
    )[0].reshape(channels, volume)
    fields = jnp.maximum(total + conv_bias[:, None], 0.0).astype(jnp.bfloat16)
    pair_count = pair_edge.shape[0]
    slot_count = pair_count * BINS
    slots_flat = voxel_slot.reshape(volume)
    block_width = 512
    pieces = []
    for block in range(slot_count // block_width):
        labels = block * block_width + lax.iota(jnp.int32, block_width)
        onehot = (slots_flat[:, None] == labels[None, :]).astype(jnp.bfloat16)
        pieces.append(jnp.dot(fields, onehot, preferred_element_type=jnp.float32))
    pooled = jnp.concatenate(pieces, axis=1) * (slot_count / volume)
    row_width = BINS * channels
    pair_rows = (
        pooled.reshape(channels, BINS, pair_count)
        .transpose(2, 1, 0)
        .reshape(pair_count, row_width)
        .astype(jnp.bfloat16)
    )
    owners = pair_owner[:, 0]
    labels = jnp.concatenate([owners, pair_edge]).astype(jnp.bfloat16).reshape(1, row_width)
    send = jnp.concatenate([pair_rows, labels], axis=0)
    gathered = lax.all_gather(send, ("gx", "gy"), axis=0, tiled=False)
    all_rows = gathered[:, :pair_count, :].reshape(-1, row_width)
    all_labels = gathered[:, pair_count, :].astype(jnp.int32)
    all_keys = (all_labels[:, :pair_count] * EDGE_DEV + all_labels[:, pair_count:]).reshape(-1)
    keys = owners * EDGE_DEV + pair_edge
    edge_onehot = (keys[:, None] == all_keys[None, :]).astype(jnp.bfloat16)
    edge_rows = jnp.dot(edge_onehot, all_rows, preferred_element_type=jnp.float32).astype(
        jnp.bfloat16
    )
    first = jax.nn.silu(
        jnp.dot(edge_rows, mlp_in, preferred_element_type=jnp.float32) + mlp_in_bias
    ).astype(jnp.bfloat16)
    second = jax.nn.silu(
        jnp.dot(first, mlp_mid, preferred_element_type=jnp.float32) + mlp_mid_bias
    ).astype(jnp.bfloat16)
    return jnp.dot(second, mlp_out, preferred_element_type=jnp.float32)


def solution(mesh):
    placed = (
        P(None, "gx", "gy", "gz"),
        P("gx", "gy", "gz"),
        P(),
        P(),
        P(("gx", "gy", "gz"), None),
        P(("gx", "gy", "gz")),
        P(),
        P(),
        P(),
        P(),
        P(),
    )
    return jax.shard_map(
        body, mesh=mesh, in_specs=placed, out_specs=P(("gx", "gy", "gz")), check_vma=False
    )
```

```python
import jax
import jax.numpy as jnp
from jax import lax
from jax.sharding import PartitionSpec as P

BINS = 8
EDGE_DEV = 64


def extended(cells, sides, width):
    for axis, dim in sides:
        count = lax.axis_size(axis)
        ends = count - 1
        head = lax.slice_in_dim(cells, 0, width, axis=dim)
        tail = lax.slice_in_dim(cells, cells.shape[dim] - width, cells.shape[dim], axis=dim)
        cells = jnp.concatenate(
            [
                lax.ppermute(tail, axis, [(i, (i + 1) % count) for i in range(ends)]),
                cells,
                lax.ppermute(head, axis, [((i + 1) % count, i) for i in range(ends)]),
            ],
            axis=dim,
        )
    return cells


def body(
    features,
    voxel_slot,
    conv_weight,
    conv_bias,
    pair_owner,
    pair_edge,
    mlp_in,
    mlp_in_bias,
    mlp_mid,
    mlp_mid_bias,
    mlp_out,
):
    channels, extent_x, extent_y, extent_z = features.shape
    volume = extent_x * extent_y * extent_z
    cells = features.transpose(1, 2, 3, 0)
    padded = extended(cells, (("gx", 0), ("gy", 1), ("gz", 2)), 1)
    kernel = conv_weight.reshape(3, 3, 3, channels, channels).transpose(0, 1, 2, 4, 3)
    total = lax.conv_general_dilated(
        padded[None],
        kernel,
        (1, 1, 1),
        "VALID",
        dimension_numbers=("NDHWC", "DHWIO", "NDHWC"),
        preferred_element_type=jnp.float32,
    )[0].reshape(volume, channels)
    fields = jnp.maximum(total + conv_bias[None, :], 0.0).astype(jnp.bfloat16)
    pair_count = pair_edge.shape[0]
    slot_count = pair_count * BINS
    slots_flat = voxel_slot.reshape(volume)
    onehot = (slots_flat[:, None] == lax.iota(jnp.int32, slot_count)[None, :]).astype(jnp.bfloat16)
    pooled = lax.dot_general(
        onehot, fields, (((0,), (0,)), ((), ())), preferred_element_type=jnp.float32
    ) * (slot_count / volume)
    row_width = BINS * channels
    pair_rows = (
        pooled.reshape(BINS, pair_count, channels)
        .transpose(1, 0, 2)
        .reshape(pair_count, row_width)
        .astype(jnp.bfloat16)
    )
    size_gx = lax.axis_size("gx")
    size_gy = lax.axis_size("gy")
    groups = size_gx * size_gy
    capacity = max(2, (5 * pair_count + 2 * groups - 1) // (2 * groups))
    owners = pair_owner[:, 0]
    owner_marks = (owners[:, None] == lax.iota(jnp.int32, groups)[None, :]).astype(jnp.int32)
    earlier = jnp.cumsum(owner_marks, axis=0) - owner_marks
    slot_rank = jnp.sum(earlier * owner_marks, axis=1)
    target = owners * capacity + slot_rank
    send_rows = jnp.zeros((groups * capacity, row_width), jnp.bfloat16).at[target].set(pair_rows)
    send_ids = jnp.full((groups * capacity,), -1, jnp.bfloat16).at[target].set(
        pair_edge.astype(jnp.bfloat16)
    )
    id_row = jnp.pad(send_ids.reshape(groups, 1, capacity), ((0, 0), (0, 0), (0, row_width - capacity)))
    send = jnp.concatenate([send_rows.reshape(groups, capacity, row_width), id_row], axis=1)
    edge_count = EDGE_DEV
    recv = lax.all_to_all(send, ("gx", "gy"), split_axis=0, concat_axis=0, tiled=True)
    flat_rows = recv[:, :capacity, :].reshape(groups * capacity, row_width)
    flat_ids = recv[:, capacity, :capacity].reshape(groups * capacity).astype(jnp.int32)
    edge_onehot = (lax.iota(jnp.int32, edge_count)[:, None] == flat_ids[None, :]).astype(
        jnp.bfloat16
    )
    edge_rows = jnp.dot(edge_onehot, flat_rows, preferred_element_type=jnp.float32).astype(
        jnp.bfloat16
    )
    first = jax.nn.silu(
        jnp.dot(edge_rows, mlp_in, preferred_element_type=jnp.float32) + mlp_in_bias
    ).astype(jnp.bfloat16)
    second = jax.nn.silu(
        jnp.dot(first, mlp_mid, preferred_element_type=jnp.float32) + mlp_mid_bias
    ).astype(jnp.bfloat16)
    edge_scores = jnp.dot(second, mlp_out, preferred_element_type=jnp.float32)
    owner_picks = flat_ids[:, None] == lax.iota(jnp.int32, edge_count)[None, :]
    owner_scores = jnp.sum(jnp.where(owner_picks, edge_scores[None, :], 0.0), axis=1)
    returned = lax.all_to_all(
        owner_scores.reshape(groups, capacity), ("gx", "gy"), split_axis=0, concat_axis=0, tiled=True
    ).reshape(groups * capacity)
    back_picks = target[:, None] == lax.iota(jnp.int32, groups * capacity)[None, :]
    return jnp.sum(jnp.where(back_picks, returned[None, :], 0.0), axis=1)


def solution(mesh):
    placed = (
        P(None, "gx", "gy", "gz"),
        P("gx", "gy", "gz"),
        P(),
        P(),
        P(("gx", "gy", "gz"), None),
        P(("gx", "gy", "gz")),
        P(),
        P(),
        P(),
        P(),
        P(),
    )
    return jax.shard_map(
        body, mesh=mesh, in_specs=placed, out_specs=P(("gx", "gy", "gz")), check_vma=False
    )
```

```python
import jax
import numpy as np
import jax.numpy as jnp
from jax import lax
from jax.sharding import PartitionSpec as P

BINS = 8
EDGE_DEV = 64


def extended(cells, sides, width):
    for axis, dim in sides:
        count = lax.axis_size(axis)
        ends = count - 1
        head = lax.slice_in_dim(cells, 0, width, axis=dim)
        tail = lax.slice_in_dim(cells, cells.shape[dim] - width, cells.shape[dim], axis=dim)
        cells = jnp.concatenate(
            [
                lax.ppermute(tail, axis, [(i, (i + 1) % count) for i in range(ends)]),
                cells,
                lax.ppermute(head, axis, [((i + 1) % count, i) for i in range(ends)]),
            ],
            axis=dim,
        )
    return cells


def band_selector():
    sel = np.zeros((3, 4, 4, 3), np.float32)
    sel[0, 3, 0, 0] = 1.0
    for zi in range(4):
        for zo in range(4):
            if abs(zi - zo) <= 1:
                sel[1, zi, zo, zi - zo + 1] = 1.0
    sel[2, 0, 3, 2] = 1.0
    return sel


def banded_weight(conv_weight, channels):
    taps = conv_weight.astype(jnp.float32).reshape(3, 3, 3, channels, channels).transpose(0, 1, 2, 4, 3)
    full = jnp.einsum("pizd,xydco->xypiczo", band_selector(), taps, precision=lax.Precision.HIGHEST)
    return full.reshape(27 * 4 * channels, 4 * channels).astype(jnp.bfloat16)


def conv_lane_dense(padded_xy, low, high, conv_weight, channels):
    px, py, lanes = padded_xy.shape
    chunk = 4 * channels
    nchunk = lanes // chunk
    low_chunk = jnp.pad(low, ((0, 0), (0, 0), (chunk - channels, 0)))[:, :, None]
    high_chunk = jnp.pad(high, ((0, 0), (0, 0), (0, chunk - channels)))[:, :, None]
    full = jnp.concatenate([low_chunk, padded_xy.reshape(px, py, nchunk, chunk), high_chunk], axis=2)
    slabs = [
        full[dx : dx + px - 2, dy : dy + py - 2, p : p + nchunk, :]
        for dx in range(3)
        for dy in range(3)
        for p in range(3)
    ]
    stacked = jnp.concatenate(slabs, axis=3)
    return jnp.dot(stacked, banded_weight(conv_weight, channels), preferred_element_type=jnp.float32)


def body(
    features,
    voxel_slot,
    conv_weight,
    conv_bias,
    pair_owner,
    pair_edge,
    mlp_in,
    mlp_in_bias,
    mlp_mid,
    mlp_mid_bias,
    mlp_out,
):
    channels, extent_x, extent_y, extent_z = features.shape
    volume = extent_x * extent_y * extent_z
    cells = features.transpose(1, 2, 3, 0).reshape(extent_x, extent_y, extent_z * channels)
    padded = extended(cells, (("gx", 0), ("gy", 1)), 1)
    count_z = lax.axis_size("gz")
    low = lax.ppermute(
        padded[:, :, -channels:], "gz", [(i, i + 1) for i in range(count_z - 1)]
    )
    high = lax.ppermute(
        padded[:, :, :channels], "gz", [(i + 1, i) for i in range(count_z - 1)]
    )
    total = conv_lane_dense(padded, low, high, conv_weight, channels).reshape(volume, channels)
    fields = jnp.maximum(total + conv_bias[None, :], 0.0).astype(jnp.bfloat16)
    pair_count = pair_edge.shape[0]
    slot_count = pair_count * BINS
    slots_flat = voxel_slot.reshape(volume)
    onehot = (slots_flat[:, None] == lax.iota(jnp.int32, slot_count)[None, :]).astype(jnp.bfloat16)
    pooled = lax.dot_general(
        onehot, fields, (((0,), (0,)), ((), ())), preferred_element_type=jnp.float32
    ) * (slot_count / volume)
    row_width = BINS * channels
    pair_rows = (
        pooled.reshape(BINS, pair_count, channels)
        .transpose(1, 0, 2)
        .reshape(pair_count, row_width)
        .astype(jnp.bfloat16)
    )
    size_gx = lax.axis_size("gx")
    size_gy = lax.axis_size("gy")
    groups = size_gx * size_gy
    capacity = max(2, (5 * pair_count + 2 * groups - 1) // (2 * groups))
    owners = pair_owner[:, 0]
    owner_marks = (owners[:, None] == lax.iota(jnp.int32, groups)[None, :]).astype(jnp.int32)
    earlier = jnp.cumsum(owner_marks, axis=0) - owner_marks
    slot_rank = jnp.sum(earlier * owner_marks, axis=1)
    target = owners * capacity + slot_rank
    send_rows = jnp.zeros((groups * capacity, row_width), jnp.bfloat16).at[target].set(pair_rows)
    send_ids = jnp.full((groups * capacity,), -1, jnp.bfloat16).at[target].set(
        pair_edge.astype(jnp.bfloat16)
    )
    id_row = jnp.pad(send_ids.reshape(groups, 1, capacity), ((0, 0), (0, 0), (0, row_width - capacity)))
    send = jnp.concatenate([send_rows.reshape(groups, capacity, row_width), id_row], axis=1)
    edge_count = EDGE_DEV
    recv = lax.all_to_all(send, ("gx", "gy"), split_axis=0, concat_axis=0, tiled=True)
    flat_rows = recv[:, :capacity, :].reshape(groups * capacity, row_width)
    flat_ids = recv[:, capacity, :capacity].reshape(groups * capacity).astype(jnp.int32)
    edge_onehot = (lax.iota(jnp.int32, edge_count)[:, None] == flat_ids[None, :]).astype(
        jnp.bfloat16
    )
    edge_rows = jnp.dot(edge_onehot, flat_rows, preferred_element_type=jnp.float32).astype(
        jnp.bfloat16
    )
    first = jax.nn.silu(
        jnp.dot(edge_rows, mlp_in, preferred_element_type=jnp.float32) + mlp_in_bias
    ).astype(jnp.bfloat16)
    second = jax.nn.silu(
        jnp.dot(first, mlp_mid, preferred_element_type=jnp.float32) + mlp_mid_bias
    ).astype(jnp.bfloat16)
    edge_scores = jnp.dot(second, mlp_out, preferred_element_type=jnp.float32)
    owner_picks = flat_ids[:, None] == lax.iota(jnp.int32, edge_count)[None, :]
    owner_scores = jnp.sum(jnp.where(owner_picks, edge_scores[None, :], 0.0), axis=1)
    returned = lax.all_to_all(
        owner_scores.reshape(groups, capacity), ("gx", "gy"), split_axis=0, concat_axis=0, tiled=True
    ).reshape(groups * capacity)
    back_picks = target[:, None] == lax.iota(jnp.int32, groups * capacity)[None, :]
    return jnp.sum(jnp.where(back_picks, returned[None, :], 0.0), axis=1)


def solution(mesh):
    placed = (
        P(None, "gx", "gy", "gz"),
        P("gx", "gy", "gz"),
        P(),
        P(),
        P(("gx", "gy", "gz"), None),
        P(("gx", "gy", "gz")),
        P(),
        P(),
        P(),
        P(),
        P(),
    )
    return jax.shard_map(
        body, mesh=mesh, in_specs=placed, out_specs=P(("gx", "gy", "gz")), check_vma=False
    )
```

```python
import jax
import numpy as np
import jax.numpy as jnp
from jax import lax
from jax.sharding import PartitionSpec as P

BINS = 8
EDGE_DEV = 64


def extended(cells, sides, width):
    for axis, dim in sides:
        count = lax.axis_size(axis)
        ends = count - 1
        head = lax.slice_in_dim(cells, 0, width, axis=dim)
        tail = lax.slice_in_dim(cells, cells.shape[dim] - width, cells.shape[dim], axis=dim)
        cells = jnp.concatenate(
            [
                lax.ppermute(tail, axis, [(i, (i + 1) % count) for i in range(ends)]),
                cells,
                lax.ppermute(head, axis, [((i + 1) % count, i) for i in range(ends)]),
            ],
            axis=dim,
        )
    return cells


def band_selector():
    sel = np.zeros((3, 4, 4, 3), np.float32)
    sel[0, 3, 0, 0] = 1.0
    for zi in range(4):
        for zo in range(4):
            if abs(zi - zo) <= 1:
                sel[1, zi, zo, zi - zo + 1] = 1.0
    sel[2, 0, 3, 2] = 1.0
    return sel


def banded_weight(conv_weight, channels):
    taps = conv_weight.astype(jnp.float32).reshape(3, 3, 3, channels, channels).transpose(0, 1, 2, 4, 3)
    full = jnp.einsum("pizd,xydco->xypiczo", band_selector(), taps, precision=lax.Precision.HIGHEST)
    return full.reshape(27 * 4 * channels, 4 * channels).astype(jnp.bfloat16)


def conv_lane_dense(padded, low, high, conv_weight, channels):
    px, py, nchunk, chunk = padded.shape
    low_chunk = jnp.pad(low, ((0, 0), (0, 0), (chunk - channels, 0)))[:, :, None]
    high_chunk = jnp.pad(high, ((0, 0), (0, 0), (0, chunk - channels)))[:, :, None]
    parts = (
        jnp.concatenate([low_chunk, padded[:, :, :-1]], axis=2),
        padded,
        jnp.concatenate([padded[:, :, 1:], high_chunk], axis=2),
    )
    slabs = [
        parts[p][dx : dx + px - 2, dy : dy + py - 2]
        for dx in range(3)
        for dy in range(3)
        for p in range(3)
    ]
    stacked = jnp.concatenate(slabs, axis=3)
    return jnp.dot(stacked, banded_weight(conv_weight, channels), preferred_element_type=jnp.float32)

def body(
    features,
    voxel_slot,
    conv_weight,
    conv_bias,
    pair_owner,
    pair_edge,
    mlp_in,
    mlp_in_bias,
    mlp_mid,
    mlp_mid_bias,
    mlp_out,
):
    channels, extent_x, extent_y, extent_z = features.shape
    volume = extent_x * extent_y * extent_z
    chunk = 4 * channels
    cells = (
        features.reshape(channels, extent_x, extent_y, extent_z // 4, 4)
        .transpose(1, 2, 3, 4, 0)
        .reshape(extent_x, extent_y, extent_z // 4, chunk)
    )
    padded = extended(cells, (("gx", 0), ("gy", 1)), 1)
    count_z = lax.axis_size("gz")
    low = lax.ppermute(
        padded[:, :, -1, chunk - channels :], "gz", [(i, i + 1) for i in range(count_z - 1)]
    )
    high = lax.ppermute(padded[:, :, 0, :channels], "gz", [(i + 1, i) for i in range(count_z - 1)])
    total = conv_lane_dense(padded, low, high, conv_weight, channels).reshape(volume, channels)
    fields = jnp.maximum(total + conv_bias[None, :], 0.0).astype(jnp.bfloat16)
    pair_count = pair_edge.shape[0]
    slot_count = pair_count * BINS
    slots_flat = voxel_slot.reshape(volume)
    onehot = (slots_flat[:, None] == lax.iota(jnp.int32, slot_count)[None, :]).astype(jnp.bfloat16)
    pooled = lax.dot_general(
        onehot, fields, (((0,), (0,)), ((), ())), preferred_element_type=jnp.float32
    ) * (slot_count / volume)
    row_width = BINS * channels
    pair_rows = (
        pooled.reshape(BINS, pair_count, channels)
        .transpose(1, 0, 2)
        .reshape(pair_count, row_width)
        .astype(jnp.bfloat16)
    )
    size_gx = lax.axis_size("gx")
    size_gy = lax.axis_size("gy")
    groups = size_gx * size_gy
    capacity = max(2, (5 * pair_count + 2 * groups - 1) // (2 * groups))
    owners = pair_owner[:, 0]
    owner_marks = (owners[:, None] == lax.iota(jnp.int32, groups)[None, :]).astype(jnp.int32)
    earlier = jnp.cumsum(owner_marks, axis=0) - owner_marks
    slot_rank = jnp.sum(earlier * owner_marks, axis=1)
    target = owners * capacity + slot_rank
    send_rows = jnp.zeros((groups * capacity, row_width), jnp.bfloat16).at[target].set(pair_rows)
    send_ids = jnp.full((groups * capacity,), -1, jnp.bfloat16).at[target].set(
        pair_edge.astype(jnp.bfloat16)
    )
    id_row = jnp.pad(send_ids.reshape(groups, 1, capacity), ((0, 0), (0, 0), (0, row_width - capacity)))
    send = jnp.concatenate([send_rows.reshape(groups, capacity, row_width), id_row], axis=1)
    edge_count = EDGE_DEV
    recv = lax.all_to_all(send, ("gx", "gy"), split_axis=0, concat_axis=0, tiled=True)
    flat_rows = recv[:, :capacity, :].reshape(groups * capacity, row_width)
    flat_ids = recv[:, capacity, :capacity].reshape(groups * capacity).astype(jnp.int32)
    edge_onehot = (lax.iota(jnp.int32, edge_count)[:, None] == flat_ids[None, :]).astype(
        jnp.bfloat16
    )
    edge_rows = jnp.dot(edge_onehot, flat_rows, preferred_element_type=jnp.float32).astype(
        jnp.bfloat16
    )
    first = jax.nn.silu(
        jnp.dot(edge_rows, mlp_in, preferred_element_type=jnp.float32) + mlp_in_bias
    ).astype(jnp.bfloat16)
    second = jax.nn.silu(
        jnp.dot(first, mlp_mid, preferred_element_type=jnp.float32) + mlp_mid_bias
    ).astype(jnp.bfloat16)
    edge_scores = jnp.dot(second, mlp_out, preferred_element_type=jnp.float32)
    owner_picks = flat_ids[:, None] == lax.iota(jnp.int32, edge_count)[None, :]
    owner_scores = jnp.sum(jnp.where(owner_picks, edge_scores[None, :], 0.0), axis=1)
    returned = lax.all_to_all(
        owner_scores.reshape(groups, capacity), ("gx", "gy"), split_axis=0, concat_axis=0, tiled=True
    ).reshape(groups * capacity)
    back_picks = target[:, None] == lax.iota(jnp.int32, groups * capacity)[None, :]
    return jnp.sum(jnp.where(back_picks, returned[None, :], 0.0), axis=1)


def solution(mesh):
    placed = (
        P(None, "gx", "gy", "gz"),
        P("gx", "gy", "gz"),
        P(),
        P(),
        P(("gx", "gy", "gz"), None),
        P(("gx", "gy", "gz")),
        P(),
        P(),
        P(),
        P(),
        P(),
    )
    return jax.shard_map(
        body, mesh=mesh, in_specs=placed, out_specs=P(("gx", "gy", "gz")), check_vma=False
    )
```

```python
import jax
import jax.numpy as jnp
from jax import lax
from jax.sharding import PartitionSpec as P

BINS = 8
EDGE_DEV = 64


def extended(cells, sides, width):
    for axis, dim in sides:
        count = lax.axis_size(axis)
        ends = count - 1
        head = lax.slice_in_dim(cells, 0, width, axis=dim)
        tail = lax.slice_in_dim(cells, cells.shape[dim] - width, cells.shape[dim], axis=dim)
        cells = jnp.concatenate(
            [
                lax.ppermute(tail, axis, [(i, (i + 1) % count) for i in range(ends)]),
                cells,
                lax.ppermute(head, axis, [((i + 1) % count, i) for i in range(ends)]),
            ],
            axis=dim,
        )
    return cells


def banded_weight(conv_weight, channels):
    taps = conv_weight.reshape(3, 3, 3, channels, channels).transpose(0, 1, 2, 4, 3)
    empty = jnp.zeros((3, 3, channels, channels), conv_weight.dtype)

    def block(part, zi, zo):
        shift = zi - zo if part == 1 else (-1 if (part, zi, zo) == (0, 3, 0) else None)
        if part == 2 and (zi, zo) == (0, 3):
            shift = 1
        if shift is None or abs(shift) > 1:
            return empty
        return taps[:, :, shift + 1]

    parts = [
        jnp.concatenate(
            [jnp.concatenate([block(part, zi, zo) for zo in range(4)], axis=3) for zi in range(4)],
            axis=2,
        )
        for part in range(3)
    ]
    return jnp.stack(parts, axis=2).reshape(27 * 4 * channels, 4 * channels)


def conv_lane_dense(padded, low, high, conv_weight, channels):
    px, py, nchunk, chunk = padded.shape
    low_chunk = jnp.pad(low, ((0, 0), (0, 0), (chunk - channels, 0)))[:, :, None]
    high_chunk = jnp.pad(high, ((0, 0), (0, 0), (0, chunk - channels)))[:, :, None]
    parts = (
        jnp.concatenate([low_chunk, padded[:, :, :-1]], axis=2),
        padded,
        jnp.concatenate([padded[:, :, 1:], high_chunk], axis=2),
    )
    slabs = [
        parts[p][dx : dx + px - 2, dy : dy + py - 2]
        for dx in range(3)
        for dy in range(3)
        for p in range(3)
    ]
    stacked = jnp.concatenate(slabs, axis=3)
    return jnp.dot(stacked, banded_weight(conv_weight, channels), preferred_element_type=jnp.float32)

def body(
    features,
    voxel_slot,
    conv_weight,
    conv_bias,
    pair_owner,
    pair_edge,
    mlp_in,
    mlp_in_bias,
    mlp_mid,
    mlp_mid_bias,
    mlp_out,
):
    channels, extent_x, extent_y, extent_z = features.shape
    volume = extent_x * extent_y * extent_z
    chunk = 4 * channels
    cells = (
        features.reshape(channels, extent_x, extent_y, extent_z // 4, 4)
        .transpose(1, 2, 3, 4, 0)
        .reshape(extent_x, extent_y, extent_z // 4, chunk)
    )
    padded = extended(cells, (("gx", 0), ("gy", 1)), 1)
    count_z = lax.axis_size("gz")
    low = lax.ppermute(
        padded[:, :, -1, chunk - channels :], "gz", [(i, i + 1) for i in range(count_z - 1)]
    )
    high = lax.ppermute(padded[:, :, 0, :channels], "gz", [(i + 1, i) for i in range(count_z - 1)])
    total = conv_lane_dense(padded, low, high, conv_weight, channels).reshape(volume, channels)
    fields = jnp.maximum(total + conv_bias[None, :], 0.0).astype(jnp.bfloat16)
    pair_count = pair_edge.shape[0]
    slot_count = pair_count * BINS
    slots_flat = voxel_slot.reshape(volume)
    onehot = (slots_flat[:, None] == lax.iota(jnp.int32, slot_count)[None, :]).astype(jnp.bfloat16)
    pooled = lax.dot_general(
        onehot, fields, (((0,), (0,)), ((), ())), preferred_element_type=jnp.float32
    ) * (slot_count / volume)
    row_width = BINS * channels
    pair_rows = (
        pooled.reshape(BINS, pair_count, channels)
        .transpose(1, 0, 2)
        .reshape(pair_count, row_width)
        .astype(jnp.bfloat16)
    )
    size_gx = lax.axis_size("gx")
    size_gy = lax.axis_size("gy")
    groups = size_gx * size_gy
    capacity = max(2, (5 * pair_count + 2 * groups - 1) // (2 * groups))
    owners = pair_owner[:, 0]
    owner_marks = (owners[:, None] == lax.iota(jnp.int32, groups)[None, :]).astype(jnp.int32)
    earlier = jnp.cumsum(owner_marks, axis=0) - owner_marks
    slot_rank = jnp.sum(earlier * owner_marks, axis=1)
    target = owners * capacity + slot_rank
    send_rows = jnp.zeros((groups * capacity, row_width), jnp.bfloat16).at[target].set(pair_rows)
    send_ids = jnp.full((groups * capacity,), -1, jnp.bfloat16).at[target].set(
        pair_edge.astype(jnp.bfloat16)
    )
    id_row = jnp.pad(send_ids.reshape(groups, 1, capacity), ((0, 0), (0, 0), (0, row_width - capacity)))
    send = jnp.concatenate([send_rows.reshape(groups, capacity, row_width), id_row], axis=1)
    edge_count = EDGE_DEV
    recv = lax.all_to_all(send, ("gx", "gy"), split_axis=0, concat_axis=0, tiled=True)
    flat_rows = recv[:, :capacity, :].reshape(groups * capacity, row_width)
    flat_ids = recv[:, capacity, :capacity].reshape(groups * capacity).astype(jnp.int32)
    edge_onehot = (lax.iota(jnp.int32, edge_count)[:, None] == flat_ids[None, :]).astype(
        jnp.bfloat16
    )
    edge_rows = jnp.dot(edge_onehot, flat_rows, preferred_element_type=jnp.float32).astype(
        jnp.bfloat16
    )
    first = jax.nn.silu(
        jnp.dot(edge_rows, mlp_in, preferred_element_type=jnp.float32) + mlp_in_bias
    ).astype(jnp.bfloat16)
    second = jax.nn.silu(
        jnp.dot(first, mlp_mid, preferred_element_type=jnp.float32) + mlp_mid_bias
    ).astype(jnp.bfloat16)
    edge_scores = jnp.dot(second, mlp_out, preferred_element_type=jnp.float32)
    owner_picks = flat_ids[:, None] == lax.iota(jnp.int32, edge_count)[None, :]
    owner_scores = jnp.sum(jnp.where(owner_picks, edge_scores[None, :], 0.0), axis=1)
    returned = lax.all_to_all(
        owner_scores.reshape(groups, capacity), ("gx", "gy"), split_axis=0, concat_axis=0, tiled=True
    ).reshape(groups * capacity)
    back_picks = target[:, None] == lax.iota(jnp.int32, groups * capacity)[None, :]
    return jnp.sum(jnp.where(back_picks, returned[None, :], 0.0), axis=1)


def solution(mesh):
    placed = (
        P(None, "gx", "gy", "gz"),
        P("gx", "gy", "gz"),
        P(),
        P(),
        P(("gx", "gy", "gz"), None),
        P(("gx", "gy", "gz")),
        P(),
        P(),
        P(),
        P(),
        P(),
    )
    return jax.shard_map(
        body, mesh=mesh, in_specs=placed, out_specs=P(("gx", "gy", "gz")), check_vma=False
    )
```

```python
import jax
import jax.numpy as jnp
from jax import lax
from jax.sharding import PartitionSpec as P

BINS = 8
EDGE_DEV = 64


def extended(cells, sides, width):
    for axis, dim in sides:
        count = lax.axis_size(axis)
        ends = count - 1
        head = lax.slice_in_dim(cells, 0, width, axis=dim)
        tail = lax.slice_in_dim(cells, cells.shape[dim] - width, cells.shape[dim], axis=dim)
        cells = jnp.concatenate(
            [
                lax.ppermute(tail, axis, [(i, (i + 1) % count) for i in range(ends)]),
                cells,
                lax.ppermute(head, axis, [((i + 1) % count, i) for i in range(ends)]),
            ],
            axis=dim,
        )
    return cells


def banded_weight(conv_weight, channels):
    taps = conv_weight.reshape(3, 3, 3, channels, channels).transpose(0, 1, 2, 4, 3)
    empty = jnp.zeros((3, 3, channels, channels), conv_weight.dtype)

    def block(part, zi, zo):
        shift = zi - zo if part == 1 else (-1 if (part, zi, zo) == (0, 3, 0) else None)
        if part == 2 and (zi, zo) == (0, 3):
            shift = 1
        if shift is None or abs(shift) > 1:
            return empty
        return taps[:, :, shift + 1]

    parts = [
        jnp.concatenate(
            [jnp.concatenate([block(part, zi, zo) for zo in range(4)], axis=3) for zi in range(4)],
            axis=2,
        )
        for part in range(3)
    ]
    return jnp.stack(parts, axis=2).reshape(27 * 4 * channels, 4 * channels)


def conv_lane_dense(padded, low, high, conv_weight, channels):
    px, py, nchunk, chunk = padded.shape
    weight = banded_weight(conv_weight, channels)
    blocks = weight.reshape(9, 3, chunk, chunk)
    empty = jnp.zeros((px, py, 1, chunk), padded.dtype)
    parts = (
        jnp.concatenate([empty, padded[:, :, :-1]], axis=2),
        padded,
        jnp.concatenate([padded[:, :, 1:], empty], axis=2),
    )
    slabs = [
        parts[p][dx : dx + px - 2, dy : dy + py - 2]
        for dx in range(3)
        for dy in range(3)
        for p in range(3)
    ]
    main = jnp.dot(jnp.concatenate(slabs, axis=3), weight, preferred_element_type=jnp.float32)
    low_chunk = jnp.pad(low, ((0, 0), (0, 0), (chunk - channels, 0)))
    high_chunk = jnp.pad(high, ((0, 0), (0, 0), (0, chunk - channels)))

    def edge(halo, part):
        pieces = [halo[dx : dx + px - 2, dy : dy + py - 2] for dx in range(3) for dy in range(3)]
        return jnp.dot(
            jnp.concatenate(pieces, axis=2),
            blocks[:, part].reshape(9 * chunk, chunk),
            preferred_element_type=jnp.float32,
        )

    main = main.at[:, :, 0, :].add(edge(low_chunk, 0))
    return main.at[:, :, nchunk - 1, :].add(edge(high_chunk, 2))

def body(
    features,
    voxel_slot,
    conv_weight,
    conv_bias,
    pair_owner,
    pair_edge,
    mlp_in,
    mlp_in_bias,
    mlp_mid,
    mlp_mid_bias,
    mlp_out,
):
    channels, extent_x, extent_y, extent_z = features.shape
    volume = extent_x * extent_y * extent_z
    chunk = 4 * channels
    cells = (
        features.reshape(channels, extent_x, extent_y, extent_z // 4, 4)
        .transpose(1, 2, 3, 4, 0)
        .reshape(extent_x, extent_y, extent_z // 4, chunk)
    )
    padded = extended(cells, (("gx", 0), ("gy", 1)), 1)
    count_z = lax.axis_size("gz")
    low = lax.ppermute(
        padded[:, :, -1, chunk - channels :], "gz", [(i, i + 1) for i in range(count_z - 1)]
    )
    high = lax.ppermute(padded[:, :, 0, :channels], "gz", [(i + 1, i) for i in range(count_z - 1)])
    total = conv_lane_dense(padded, low, high, conv_weight, channels).reshape(volume, channels)
    fields = jnp.maximum(total + conv_bias[None, :], 0.0).astype(jnp.bfloat16)
    pair_count = pair_edge.shape[0]
    slot_count = pair_count * BINS
    slots_flat = voxel_slot.reshape(volume)
    onehot = (slots_flat[:, None] == lax.iota(jnp.int32, slot_count)[None, :]).astype(jnp.bfloat16)
    pooled = lax.dot_general(
        onehot, fields, (((0,), (0,)), ((), ())), preferred_element_type=jnp.float32
    ) * (slot_count / volume)
    row_width = BINS * channels
    pair_rows = (
        pooled.reshape(BINS, pair_count, channels)
        .transpose(1, 0, 2)
        .reshape(pair_count, row_width)
        .astype(jnp.bfloat16)
    )
    size_gx = lax.axis_size("gx")
    size_gy = lax.axis_size("gy")
    groups = size_gx * size_gy
    capacity = max(2, (5 * pair_count + 2 * groups - 1) // (2 * groups))
    owners = pair_owner[:, 0]
    owner_marks = (owners[:, None] == lax.iota(jnp.int32, groups)[None, :]).astype(jnp.int32)
    earlier = jnp.cumsum(owner_marks, axis=0) - owner_marks
    slot_rank = jnp.sum(earlier * owner_marks, axis=1)
    target = owners * capacity + slot_rank
    send_rows = jnp.zeros((groups * capacity, row_width), jnp.bfloat16).at[target].set(pair_rows)
    send_ids = jnp.full((groups * capacity,), -1, jnp.bfloat16).at[target].set(
        pair_edge.astype(jnp.bfloat16)
    )
    id_row = jnp.pad(send_ids.reshape(groups, 1, capacity), ((0, 0), (0, 0), (0, row_width - capacity)))
    send = jnp.concatenate([send_rows.reshape(groups, capacity, row_width), id_row], axis=1)
    edge_count = EDGE_DEV
    recv = lax.all_to_all(send, ("gx", "gy"), split_axis=0, concat_axis=0, tiled=True)
    flat_rows = recv[:, :capacity, :].reshape(groups * capacity, row_width)
    flat_ids = recv[:, capacity, :capacity].reshape(groups * capacity).astype(jnp.int32)
    edge_onehot = (lax.iota(jnp.int32, edge_count)[:, None] == flat_ids[None, :]).astype(
        jnp.bfloat16
    )
    edge_rows = jnp.dot(edge_onehot, flat_rows, preferred_element_type=jnp.float32).astype(
        jnp.bfloat16
    )
    first = jax.nn.silu(
        jnp.dot(edge_rows, mlp_in, preferred_element_type=jnp.float32) + mlp_in_bias
    ).astype(jnp.bfloat16)
    second = jax.nn.silu(
        jnp.dot(first, mlp_mid, preferred_element_type=jnp.float32) + mlp_mid_bias
    ).astype(jnp.bfloat16)
    edge_scores = jnp.dot(second, mlp_out, preferred_element_type=jnp.float32)
    owner_picks = flat_ids[:, None] == lax.iota(jnp.int32, edge_count)[None, :]
    owner_scores = jnp.sum(jnp.where(owner_picks, edge_scores[None, :], 0.0), axis=1)
    returned = lax.all_to_all(
        owner_scores.reshape(groups, capacity), ("gx", "gy"), split_axis=0, concat_axis=0, tiled=True
    ).reshape(groups * capacity)
    back_picks = target[:, None] == lax.iota(jnp.int32, groups * capacity)[None, :]
    return jnp.sum(jnp.where(back_picks, returned[None, :], 0.0), axis=1)


def solution(mesh):
    placed = (
        P(None, "gx", "gy", "gz"),
        P("gx", "gy", "gz"),
        P(),
        P(),
        P(("gx", "gy", "gz"), None),
        P(("gx", "gy", "gz")),
        P(),
        P(),
        P(),
        P(),
        P(),
    )
    return jax.shard_map(
        body, mesh=mesh, in_specs=placed, out_specs=P(("gx", "gy", "gz")), check_vma=False
    )
```

```python
import jax
import jax.numpy as jnp
from jax import lax
from jax.sharding import PartitionSpec as P

BINS = 8
EDGE_DEV = 64


def extended(cells, sides, width):
    for axis, dim in sides:
        count = lax.axis_size(axis)
        ends = count - 1
        head = lax.slice_in_dim(cells, 0, width, axis=dim)
        tail = lax.slice_in_dim(cells, cells.shape[dim] - width, cells.shape[dim], axis=dim)
        cells = jnp.concatenate(
            [
                lax.ppermute(tail, axis, [(i, (i + 1) % count) for i in range(ends)]),
                cells,
                lax.ppermute(head, axis, [((i + 1) % count, i) for i in range(ends)]),
            ],
            axis=dim,
        )
    return cells


def banded_weight(conv_weight, channels):
    taps = conv_weight.reshape(3, 3, 3, channels, channels).transpose(0, 1, 2, 4, 3)
    empty = jnp.zeros((3, 3, channels, channels), conv_weight.dtype)

    def block(part, zi, zo):
        shift = zi - zo if part == 1 else (-1 if (part, zi, zo) == (0, 3, 0) else None)
        if part == 2 and (zi, zo) == (0, 3):
            shift = 1
        if shift is None or abs(shift) > 1:
            return empty
        return taps[:, :, shift + 1]

    parts = [
        jnp.concatenate(
            [jnp.concatenate([block(part, zi, zo) for zo in range(4)], axis=3) for zi in range(4)],
            axis=2,
        )
        for part in range(3)
    ]
    return jnp.stack(parts, axis=2).reshape(27 * 4 * channels, 4 * channels)


def conv_lane_dense(padded, low, high, conv_weight, channels):
    px, py, nchunk, chunk = padded.shape
    weight = banded_weight(conv_weight, channels)
    blocks = weight.reshape(9, 3, chunk, chunk)
    empty = jnp.zeros((px, py, 1, chunk), padded.dtype)
    parts = (
        jnp.concatenate([empty, padded[:, :, :-1]], axis=2),
        padded,
        jnp.concatenate([padded[:, :, 1:], empty], axis=2),
    )
    slabs = [
        parts[p][dx : dx + px - 2, dy : dy + py - 2]
        for dx in range(3)
        for dy in range(3)
        for p in range(3)
    ]
    main = jnp.dot(jnp.concatenate(slabs, axis=3), weight, preferred_element_type=jnp.float32)
    low_chunk = jnp.pad(low, ((0, 0), (0, 0), (chunk - channels, 0)))
    high_chunk = jnp.pad(high, ((0, 0), (0, 0), (0, chunk - channels)))

    def edge(halo, part):
        pieces = [halo[dx : dx + px - 2, dy : dy + py - 2] for dx in range(3) for dy in range(3)]
        return jnp.dot(
            jnp.concatenate(pieces, axis=2),
            blocks[:, part].reshape(9 * chunk, chunk),
            preferred_element_type=jnp.float32,
        )

    main = main.at[:, :, 0, :].add(edge(low_chunk, 0))
    return main.at[:, :, nchunk - 1, :].add(edge(high_chunk, 2))

def body(
    features,
    voxel_slot,
    conv_weight,
    conv_bias,
    pair_owner,
    pair_edge,
    mlp_in,
    mlp_in_bias,
    mlp_mid,
    mlp_mid_bias,
    mlp_out,
):
    channels, extent_x, extent_y, extent_z = features.shape
    volume = extent_x * extent_y * extent_z
    chunk = 4 * channels
    cells = (
        features.reshape(channels, extent_x, extent_y, extent_z // 4, 4)
        .transpose(1, 2, 3, 4, 0)
        .reshape(extent_x, extent_y, extent_z // 4, chunk)
    )
    padded = extended(cells, (("gx", 0), ("gy", 1)), 1)
    count_z = lax.axis_size("gz")
    low = lax.ppermute(
        padded[:, :, -1, chunk - channels :], "gz", [(i, i + 1) for i in range(count_z - 1)]
    )
    high = lax.ppermute(padded[:, :, 0, :channels], "gz", [(i + 1, i) for i in range(count_z - 1)])
    total = conv_lane_dense(padded, low, high, conv_weight, channels).reshape(volume, channels)
    fields = jnp.maximum(total + conv_bias[None, :], 0.0).astype(jnp.bfloat16)
    pair_count = pair_edge.shape[0]
    slot_count = pair_count * BINS
    slots_flat = voxel_slot.reshape(volume)
    onehot = (slots_flat[:, None] == lax.iota(jnp.int32, slot_count)[None, :]).astype(jnp.bfloat16)
    pooled = lax.dot_general(
        onehot, fields, (((0,), (0,)), ((), ())), preferred_element_type=jnp.float32
    ) * (slot_count / volume)
    row_width = BINS * channels
    pair_rows = (
        pooled.reshape(BINS, pair_count, channels)
        .transpose(1, 0, 2)
        .reshape(pair_count, row_width)
        .astype(jnp.bfloat16)
    )
    size_gx = lax.axis_size("gx")
    size_gy = lax.axis_size("gy")
    groups = size_gx * size_gy
    capacity = max(2, (5 * pair_count + 2 * groups - 1) // (2 * groups))
    capacity = max(capacity, 7)
    owners = pair_owner[:, 0]
    owner_marks = (owners[:, None] == lax.iota(jnp.int32, groups)[None, :]).astype(jnp.int32)
    earlier = jnp.cumsum(owner_marks, axis=0) - owner_marks
    slot_rank = jnp.sum(earlier * owner_marks, axis=1)
    target = owners * capacity + slot_rank
    placing = (lax.iota(jnp.int32, groups * capacity)[:, None] == target[None, :]).astype(jnp.bfloat16)
    send_rows = jnp.dot(placing, pair_rows, preferred_element_type=jnp.float32).astype(jnp.bfloat16)
    send_ids = jnp.full((groups * capacity,), -1, jnp.bfloat16).at[target].set(
        pair_edge.astype(jnp.bfloat16)
    )
    id_row = jnp.pad(send_ids.reshape(groups, 1, capacity), ((0, 0), (0, 0), (0, row_width - capacity)))
    send = jnp.concatenate([send_rows.reshape(groups, capacity, row_width), id_row], axis=1)
    edge_count = EDGE_DEV
    recv = lax.all_to_all(send, ("gx", "gy"), split_axis=0, concat_axis=0, tiled=True)
    flat_rows = recv[:, :capacity, :].reshape(groups * capacity, row_width)
    flat_ids = recv[:, capacity, :capacity].reshape(groups * capacity).astype(jnp.int32)
    edge_onehot = (lax.iota(jnp.int32, edge_count)[:, None] == flat_ids[None, :]).astype(
        jnp.bfloat16
    )
    edge_rows = jnp.dot(edge_onehot, flat_rows, preferred_element_type=jnp.float32).astype(
        jnp.bfloat16
    )
    first = jax.nn.silu(
        jnp.dot(edge_rows, mlp_in, preferred_element_type=jnp.float32) + mlp_in_bias
    ).astype(jnp.bfloat16)
    second = jax.nn.silu(
        jnp.dot(first, mlp_mid, preferred_element_type=jnp.float32) + mlp_mid_bias
    ).astype(jnp.bfloat16)
    edge_scores = jnp.dot(second, mlp_out, preferred_element_type=jnp.float32)
    owner_picks = flat_ids[:, None] == lax.iota(jnp.int32, edge_count)[None, :]
    owner_scores = jnp.sum(jnp.where(owner_picks, edge_scores[None, :], 0.0), axis=1)
    returned = lax.all_to_all(
        owner_scores.reshape(groups, capacity), ("gx", "gy"), split_axis=0, concat_axis=0, tiled=True
    ).reshape(groups * capacity)
    back_picks = target[:, None] == lax.iota(jnp.int32, groups * capacity)[None, :]
    return jnp.sum(jnp.where(back_picks, returned[None, :], 0.0), axis=1)


def solution(mesh):
    placed = (
        P(None, "gx", "gy", "gz"),
        P("gx", "gy", "gz"),
        P(),
        P(),
        P(("gx", "gy", "gz"), None),
        P(("gx", "gy", "gz")),
        P(),
        P(),
        P(),
        P(),
        P(),
    )
    return jax.shard_map(
        body, mesh=mesh, in_specs=placed, out_specs=P(("gx", "gy", "gz")), check_vma=False
    )
```

```python
import jax
import jax.numpy as jnp
from jax import lax
from jax.sharding import PartitionSpec as P

BINS = 8
EDGE_DEV = 64


def extended(cells, sides, width):
    for axis, dim in sides:
        count = lax.axis_size(axis)
        ends = count - 1
        head = lax.slice_in_dim(cells, 0, width, axis=dim)
        tail = lax.slice_in_dim(cells, cells.shape[dim] - width, cells.shape[dim], axis=dim)
        cells = jnp.concatenate(
            [
                lax.ppermute(tail, axis, [(i, (i + 1) % count) for i in range(ends)]),
                cells,
                lax.ppermute(head, axis, [((i + 1) % count, i) for i in range(ends)]),
            ],
            axis=dim,
        )
    return cells


def banded_weight(conv_weight, channels):
    taps = conv_weight.reshape(3, 3, 3, channels, channels).transpose(0, 1, 2, 4, 3)
    empty = jnp.zeros((3, 3, channels, channels), conv_weight.dtype)

    def block(part, zi, zo):
        shift = zi - zo if part == 1 else (-1 if (part, zi, zo) == (0, 3, 0) else None)
        if part == 2 and (zi, zo) == (0, 3):
            shift = 1
        if shift is None or abs(shift) > 1:
            return empty
        return taps[:, :, shift + 1]

    parts = [
        jnp.concatenate(
            [jnp.concatenate([block(part, zi, zo) for zo in range(4)], axis=3) for zi in range(4)],
            axis=2,
        )
        for part in range(3)
    ]
    return jnp.stack(parts, axis=2).reshape(27 * 4 * channels, 4 * channels)


def conv_lane_dense(padded, low, high, conv_weight, channels):
    px, py, nchunk, chunk = padded.shape
    weight = banded_weight(conv_weight, channels)
    blocks = weight.reshape(9, 3, chunk, chunk)
    empty = jnp.zeros((px, py, 1, chunk), padded.dtype)
    parts = (
        jnp.concatenate([empty, padded[:, :, :-1]], axis=2),
        padded,
        jnp.concatenate([padded[:, :, 1:], empty], axis=2),
    )
    slabs = [
        parts[p][dx : dx + px - 2, dy : dy + py - 2]
        for dx in range(3)
        for dy in range(3)
        for p in range(3)
    ]
    main = jnp.dot(jnp.concatenate(slabs, axis=3), weight, preferred_element_type=jnp.float32)
    low_chunk = jnp.pad(low, ((0, 0), (0, 0), (chunk - channels, 0)))
    high_chunk = jnp.pad(high, ((0, 0), (0, 0), (0, chunk - channels)))

    def edge(halo, part):
        pieces = [halo[dx : dx + px - 2, dy : dy + py - 2] for dx in range(3) for dy in range(3)]
        return jnp.dot(
            jnp.concatenate(pieces, axis=2),
            blocks[:, part].reshape(9 * chunk, chunk),
            preferred_element_type=jnp.float32,
        )

    main = main.at[:, :, 0, :].add(edge(low_chunk, 0))
    return main.at[:, :, nchunk - 1, :].add(edge(high_chunk, 2))

def body(
    features,
    voxel_slot,
    conv_weight,
    conv_bias,
    pair_owner,
    pair_edge,
    mlp_in,
    mlp_in_bias,
    mlp_mid,
    mlp_mid_bias,
    mlp_out,
):
    channels, extent_x, extent_y, extent_z = features.shape
    volume = extent_x * extent_y * extent_z
    chunk = 4 * channels
    cells = (
        features.reshape(channels, extent_x, extent_y, extent_z // 4, 4)
        .transpose(1, 2, 3, 4, 0)
        .reshape(extent_x, extent_y, extent_z // 4, chunk)
    )
    padded = extended(cells, (("gx", 0), ("gy", 1)), 1)
    count_z = lax.axis_size("gz")
    low = lax.ppermute(
        padded[:, :, -1, chunk - channels :], "gz", [(i, i + 1) for i in range(count_z - 1)]
    )
    high = lax.ppermute(padded[:, :, 0, :channels], "gz", [(i + 1, i) for i in range(count_z - 1)])
    total = conv_lane_dense(padded, low, high, conv_weight, channels).reshape(volume, channels)
    fields = jnp.maximum(total + conv_bias[None, :], 0.0).astype(jnp.bfloat16)
    pair_count = pair_edge.shape[0]
    slot_count = pair_count * BINS
    slots_flat = voxel_slot.reshape(volume)
    onehot = (slots_flat[:, None] == lax.iota(jnp.int32, slot_count)[None, :]).astype(jnp.bfloat16)
    pooled = lax.dot_general(
        onehot, fields, (((0,), (0,)), ((), ())), preferred_element_type=jnp.float32
    ) * (slot_count / volume)
    row_width = BINS * channels
    pair_rows = (
        pooled.reshape(BINS, pair_count, channels)
        .transpose(1, 0, 2)
        .reshape(pair_count, row_width)
        .astype(jnp.bfloat16)
    )
    size_gx = lax.axis_size("gx")
    size_gy = lax.axis_size("gy")
    groups = size_gx * size_gy
    capacity = max(2, (5 * pair_count + 2 * groups - 1) // (2 * groups))
    capacity = max(capacity, 7)
    owners = pair_owner[:, 0]
    owner_marks = (owners[:, None] == lax.iota(jnp.int32, groups)[None, :]).astype(jnp.int32)
    earlier = jnp.cumsum(owner_marks, axis=0) - owner_marks
    slot_rank = jnp.sum(earlier * owner_marks, axis=1)
    target = owners * capacity + slot_rank
    placing = (lax.iota(jnp.int32, groups * capacity)[:, None] == target[None, :]).astype(jnp.bfloat16)
    send_rows = jnp.dot(placing, pair_rows, preferred_element_type=jnp.float32).astype(jnp.bfloat16)
    send_ids = jnp.full((groups * capacity,), -1, jnp.bfloat16).at[target].set(
        pair_edge.astype(jnp.bfloat16)
    )
    id_row = jnp.pad(send_ids.reshape(groups, 1, capacity), ((0, 0), (0, 0), (0, row_width - capacity)))
    send = jnp.concatenate([send_rows.reshape(groups, capacity, row_width), id_row], axis=1)
    edge_count = EDGE_DEV
    recv = lax.all_to_all(send, ("gx", "gy"), split_axis=0, concat_axis=0, tiled=True)
    flat_rows = recv[:, :capacity, :].reshape(groups * capacity, row_width)
    flat_ids = recv[:, capacity, :capacity].reshape(groups * capacity).astype(jnp.int32)
    edge_onehot = (lax.iota(jnp.int32, edge_count)[:, None] == flat_ids[None, :]).astype(
        jnp.bfloat16
    )
    edge_rows = jnp.dot(edge_onehot, flat_rows, preferred_element_type=jnp.float32).astype(
        jnp.bfloat16
    )
    first = jax.nn.silu(
        jnp.dot(edge_rows, mlp_in, preferred_element_type=jnp.float32) + mlp_in_bias
    ).astype(jnp.bfloat16)
    second = jax.nn.silu(
        jnp.dot(first, mlp_mid, preferred_element_type=jnp.float32) + mlp_mid_bias
    ).astype(jnp.bfloat16)
    edge_scores = jnp.dot(second, mlp_out, preferred_element_type=jnp.float32)
    owner_picks = flat_ids[:, None] == lax.iota(jnp.int32, edge_count)[None, :]
    owner_scores = jnp.dot(
        owner_picks.astype(jnp.float32), edge_scores, precision=lax.Precision.HIGHEST
    )
    returned = lax.all_to_all(
        owner_scores.reshape(groups, capacity), ("gx", "gy"), split_axis=0, concat_axis=0, tiled=True
    ).reshape(groups * capacity)
    back_picks = target[:, None] == lax.iota(jnp.int32, groups * capacity)[None, :]
    return jnp.dot(back_picks.astype(jnp.float32), returned, precision=lax.Precision.HIGHEST)


def solution(mesh):
    placed = (
        P(None, "gx", "gy", "gz"),
        P("gx", "gy", "gz"),
        P(),
        P(),
        P(("gx", "gy", "gz"), None),
        P(("gx", "gy", "gz")),
        P(),
        P(),
        P(),
        P(),
        P(),
    )
    return jax.shard_map(
        body, mesh=mesh, in_specs=placed, out_specs=P(("gx", "gy", "gz")), check_vma=False
    )
```

```python
import jax
import jax.numpy as jnp
from jax import lax
from jax.sharding import PartitionSpec as P

BINS = 8
EDGE_DEV = 64


def extended(cells, sides, width):
    for axis, dim in sides:
        count = lax.axis_size(axis)
        ends = count - 1
        head = lax.slice_in_dim(cells, 0, width, axis=dim)
        tail = lax.slice_in_dim(cells, cells.shape[dim] - width, cells.shape[dim], axis=dim)
        cells = jnp.concatenate(
            [
                lax.ppermute(tail, axis, [(i, (i + 1) % count) for i in range(ends)]),
                cells,
                lax.ppermute(head, axis, [((i + 1) % count, i) for i in range(ends)]),
            ],
            axis=dim,
        )
    return cells


def banded_weight(conv_weight, channels):
    taps = conv_weight.reshape(3, 3, 3, channels, channels).transpose(0, 1, 2, 4, 3)
    empty = jnp.zeros((3, 3, channels, channels), conv_weight.dtype)

    def block(part, zi, zo):
        shift = zi - zo if part == 1 else (-1 if (part, zi, zo) == (0, 3, 0) else None)
        if part == 2 and (zi, zo) == (0, 3):
            shift = 1
        if shift is None or abs(shift) > 1:
            return empty
        return taps[:, :, shift + 1]

    parts = [
        jnp.concatenate(
            [jnp.concatenate([block(part, zi, zo) for zo in range(4)], axis=3) for zi in range(4)],
            axis=2,
        )
        for part in range(3)
    ]
    return jnp.stack(parts, axis=2).reshape(27 * 4 * channels, 4 * channels)


def conv_lane_dense(padded, low, high, conv_weight, channels):
    px, py, nchunk, chunk = padded.shape
    weight = banded_weight(conv_weight, channels)
    blocks = weight.reshape(9, 3, chunk, chunk)
    empty = jnp.zeros((px, py, 1, chunk), padded.dtype)
    parts = (
        jnp.concatenate([empty, padded[:, :, :-1]], axis=2),
        padded,
        jnp.concatenate([padded[:, :, 1:], empty], axis=2),
    )
    slabs = [
        parts[p][dx : dx + px - 2, dy : dy + py - 2]
        for dx in range(3)
        for dy in range(3)
        for p in range(3)
    ]
    main = jnp.dot(jnp.concatenate(slabs, axis=3), weight, preferred_element_type=jnp.float32)
    low_chunk = jnp.pad(low, ((0, 0), (0, 0), (chunk - channels, 0)))
    high_chunk = jnp.pad(high, ((0, 0), (0, 0), (0, chunk - channels)))

    def edge(halo, part):
        pieces = [halo[dx : dx + px - 2, dy : dy + py - 2] for dx in range(3) for dy in range(3)]
        return jnp.dot(
            jnp.concatenate(pieces, axis=2),
            blocks[:, part].reshape(9 * chunk, chunk),
            preferred_element_type=jnp.float32,
        )

    main = main.at[:, :, 0, :].add(edge(low_chunk, 0))
    return main.at[:, :, nchunk - 1, :].add(edge(high_chunk, 2))

def body(
    features,
    voxel_slot,
    conv_weight,
    conv_bias,
    pair_owner,
    pair_edge,
    mlp_in,
    mlp_in_bias,
    mlp_mid,
    mlp_mid_bias,
    mlp_out,
):
    channels, extent_x, extent_y, extent_z = features.shape
    volume = extent_x * extent_y * extent_z
    chunk = 4 * channels
    cells = (
        features.reshape(channels, extent_x, extent_y, extent_z // 4, 4)
        .transpose(1, 2, 3, 4, 0)
        .reshape(extent_x, extent_y, extent_z // 4, chunk)
    )
    padded = extended(cells, (("gx", 0), ("gy", 1)), 1)
    count_z = lax.axis_size("gz")
    low = lax.ppermute(
        padded[:, :, -1, chunk - channels :], "gz", [(i, i + 1) for i in range(count_z - 1)]
    )
    high = lax.ppermute(padded[:, :, 0, :channels], "gz", [(i + 1, i) for i in range(count_z - 1)])
    total = conv_lane_dense(padded, low, high, conv_weight, channels).reshape(volume, channels)
    fields = jnp.maximum(total + conv_bias[None, :], 0.0).astype(jnp.bfloat16)
    pair_count = pair_edge.shape[0]
    slot_count = pair_count * BINS
    slots_flat = voxel_slot.reshape(volume)
    row_width = BINS * channels
    bins = slots_flat // pair_count
    masked = jnp.where(
        bins[:, None, None] == lax.iota(jnp.int32, BINS)[None, :, None], fields[:, None, :], 0.0
    ).astype(jnp.bfloat16).reshape(volume, row_width)
    pair_onehot = (
        (slots_flat % pair_count)[:, None] == lax.iota(jnp.int32, pair_count)[None, :]
    ).astype(jnp.bfloat16)
    pooled = lax.dot_general(
        pair_onehot, masked, (((0,), (0,)), ((), ())), preferred_element_type=jnp.float32
    ) * (slot_count / volume)
    pair_rows = pooled.astype(jnp.bfloat16)
    size_gx = lax.axis_size("gx")
    size_gy = lax.axis_size("gy")
    groups = size_gx * size_gy
    capacity = max(2, (5 * pair_count + 2 * groups - 1) // (2 * groups))
    capacity = max(capacity, 7)
    owners = pair_owner[:, 0]
    owner_marks = (owners[:, None] == lax.iota(jnp.int32, groups)[None, :]).astype(jnp.int32)
    earlier = jnp.cumsum(owner_marks, axis=0) - owner_marks
    slot_rank = jnp.sum(earlier * owner_marks, axis=1)
    target = owners * capacity + slot_rank
    placing = (lax.iota(jnp.int32, groups * capacity)[:, None] == target[None, :]).astype(jnp.bfloat16)
    send_rows = jnp.dot(placing, pair_rows, preferred_element_type=jnp.float32).astype(jnp.bfloat16)
    send_ids = jnp.full((groups * capacity,), -1, jnp.bfloat16).at[target].set(
        pair_edge.astype(jnp.bfloat16)
    )
    id_row = jnp.pad(send_ids.reshape(groups, 1, capacity), ((0, 0), (0, 0), (0, row_width - capacity)))
    send = jnp.concatenate([send_rows.reshape(groups, capacity, row_width), id_row], axis=1)
    edge_count = EDGE_DEV
    recv = lax.all_to_all(send, ("gx", "gy"), split_axis=0, concat_axis=0, tiled=True)
    flat_rows = recv[:, :capacity, :].reshape(groups * capacity, row_width)
    flat_ids = recv[:, capacity, :capacity].reshape(groups * capacity).astype(jnp.int32)
    edge_onehot = (lax.iota(jnp.int32, edge_count)[:, None] == flat_ids[None, :]).astype(
        jnp.bfloat16
    )
    edge_rows = jnp.dot(edge_onehot, flat_rows, preferred_element_type=jnp.float32).astype(
        jnp.bfloat16
    )
    first = jax.nn.silu(
        jnp.dot(edge_rows, mlp_in, preferred_element_type=jnp.float32) + mlp_in_bias
    ).astype(jnp.bfloat16)
    second = jax.nn.silu(
        jnp.dot(first, mlp_mid, preferred_element_type=jnp.float32) + mlp_mid_bias
    ).astype(jnp.bfloat16)
    edge_scores = jnp.dot(second, mlp_out, preferred_element_type=jnp.float32)
    owner_picks = flat_ids[:, None] == lax.iota(jnp.int32, edge_count)[None, :]
    owner_scores = jnp.sum(jnp.where(owner_picks, edge_scores[None, :], 0.0), axis=1)
    returned = lax.all_to_all(
        owner_scores.reshape(groups, capacity), ("gx", "gy"), split_axis=0, concat_axis=0, tiled=True
    ).reshape(groups * capacity)
    back_picks = target[:, None] == lax.iota(jnp.int32, groups * capacity)[None, :]
    return jnp.sum(jnp.where(back_picks, returned[None, :], 0.0), axis=1)


def solution(mesh):
    placed = (
        P(None, "gx", "gy", "gz"),
        P("gx", "gy", "gz"),
        P(),
        P(),
        P(("gx", "gy", "gz"), None),
        P(("gx", "gy", "gz")),
        P(),
        P(),
        P(),
        P(),
        P(),
    )
    return jax.shard_map(
        body, mesh=mesh, in_specs=placed, out_specs=P(("gx", "gy", "gz")), check_vma=False
    )
```

```python
import jax
import jax.numpy as jnp
from jax import lax
from jax.sharding import PartitionSpec as P

BINS = 8
EDGE_DEV = 64


def extended(cells, sides, width):
    for axis, dim in sides:
        count = lax.axis_size(axis)
        ends = count - 1
        head = lax.slice_in_dim(cells, 0, width, axis=dim)
        tail = lax.slice_in_dim(cells, cells.shape[dim] - width, cells.shape[dim], axis=dim)
        cells = jnp.concatenate(
            [
                lax.ppermute(tail, axis, [(i, (i + 1) % count) for i in range(ends)]),
                cells,
                lax.ppermute(head, axis, [((i + 1) % count, i) for i in range(ends)]),
            ],
            axis=dim,
        )
    return cells


def banded_weight(conv_weight, channels):
    taps = conv_weight.reshape(3, 3, 3, channels, channels).transpose(0, 1, 2, 4, 3)
    empty = jnp.zeros((3, 3, channels, channels), conv_weight.dtype)

    def block(part, zi, zo):
        shift = zi - zo if part == 1 else (-1 if (part, zi, zo) == (0, 3, 0) else None)
        if part == 2 and (zi, zo) == (0, 3):
            shift = 1
        if shift is None or abs(shift) > 1:
            return empty
        return taps[:, :, shift + 1]

    parts = [
        jnp.concatenate(
            [jnp.concatenate([block(part, zi, zo) for zo in range(4)], axis=3) for zi in range(4)],
            axis=2,
        )
        for part in range(3)
    ]
    return jnp.stack(parts, axis=2).reshape(27 * 4 * channels, 4 * channels)


def conv_lane_dense(padded, low, high, conv_weight, channels):
    px, py, nchunk, chunk = padded.shape
    weight = banded_weight(conv_weight, channels)
    blocks = weight.reshape(9, 3, chunk, chunk)
    empty = jnp.zeros((px, py, 1, chunk), padded.dtype)
    parts = (
        jnp.concatenate([empty, padded[:, :, :-1]], axis=2),
        padded,
        jnp.concatenate([padded[:, :, 1:], empty], axis=2),
    )
    slabs = [
        parts[p][dx : dx + px - 2, dy : dy + py - 2]
        for dx in range(3)
        for dy in range(3)
        for p in range(3)
    ]
    main = jnp.dot(jnp.concatenate(slabs, axis=3), weight, preferred_element_type=jnp.float32)
    low_chunk = jnp.pad(low, ((0, 0), (0, 0), (chunk - channels, 0)))
    high_chunk = jnp.pad(high, ((0, 0), (0, 0), (0, chunk - channels)))

    def edge(halo, part):
        pieces = [halo[dx : dx + px - 2, dy : dy + py - 2] for dx in range(3) for dy in range(3)]
        return jnp.dot(
            jnp.concatenate(pieces, axis=2),
            blocks[:, part].reshape(9 * chunk, chunk),
            preferred_element_type=jnp.float32,
        )

    return main, edge(low_chunk, 0), edge(high_chunk, 2)

def body(
    features,
    voxel_slot,
    conv_weight,
    conv_bias,
    pair_owner,
    pair_edge,
    mlp_in,
    mlp_in_bias,
    mlp_mid,
    mlp_mid_bias,
    mlp_out,
):
    channels, extent_x, extent_y, extent_z = features.shape
    volume = extent_x * extent_y * extent_z
    chunk = 4 * channels
    cells = (
        features.reshape(channels, extent_x, extent_y, extent_z // 4, 4)
        .transpose(1, 2, 3, 4, 0)
        .reshape(extent_x, extent_y, extent_z // 4, chunk)
    )
    padded = extended(cells, (("gx", 0), ("gy", 1)), 1)
    count_z = lax.axis_size("gz")
    low = lax.ppermute(
        padded[:, :, -1, chunk - channels :], "gz", [(i, i + 1) for i in range(count_z - 1)]
    )
    high = lax.ppermute(padded[:, :, 0, :channels], "gz", [(i + 1, i) for i in range(count_z - 1)])
    main, low_fix, high_fix = conv_lane_dense(padded, low, high, conv_weight, channels)
    bias_lanes = jnp.tile(conv_bias, 4)
    chunk_index = lax.iota(jnp.int32, main.shape[2])[None, None, :, None]
    inner = (chunk_index > 0) & (chunk_index < main.shape[2] - 1)
    fields = jnp.where(inner, jnp.maximum(main + bias_lanes, 0.0), 0.0).astype(jnp.bfloat16)
    fields = fields.reshape(volume, channels)
    ends = jnp.stack(
        [main[:, :, 0] + low_fix, main[:, :, -1] + high_fix], axis=2
    )
    end_fields = jnp.maximum(ends + bias_lanes, 0.0).astype(jnp.bfloat16).reshape(-1, channels)
    pair_count = pair_edge.shape[0]
    slot_count = pair_count * BINS
    slots_flat = voxel_slot.reshape(volume)
    end_slots = voxel_slot.reshape(extent_x, extent_y, extent_z // 4, 4)[:, :, :: extent_z // 4 - 1]
    onehot = (slots_flat[:, None] == lax.iota(jnp.int32, slot_count)[None, :]).astype(jnp.bfloat16)
    end_onehot = (
        end_slots.reshape(-1)[:, None] == lax.iota(jnp.int32, slot_count)[None, :]
    ).astype(jnp.bfloat16)
    contract = (((0,), (0,)), ((), ()))
    pooled = (
        lax.dot_general(onehot, fields, contract, preferred_element_type=jnp.float32)
        + lax.dot_general(end_onehot, end_fields, contract, preferred_element_type=jnp.float32)
    ) * (slot_count / volume)
    row_width = BINS * channels
    pair_rows = (
        pooled.reshape(BINS, pair_count, channels)
        .transpose(1, 0, 2)
        .reshape(pair_count, row_width)
        .astype(jnp.bfloat16)
    )
    size_gx = lax.axis_size("gx")
    size_gy = lax.axis_size("gy")
    groups = size_gx * size_gy
    capacity = max(2, (5 * pair_count + 2 * groups - 1) // (2 * groups))
    capacity = max(capacity, 7)
    owners = pair_owner[:, 0]
    owner_marks = (owners[:, None] == lax.iota(jnp.int32, groups)[None, :]).astype(jnp.int32)
    earlier = jnp.cumsum(owner_marks, axis=0) - owner_marks
    slot_rank = jnp.sum(earlier * owner_marks, axis=1)
    target = owners * capacity + slot_rank
    placing = (lax.iota(jnp.int32, groups * capacity)[:, None] == target[None, :]).astype(jnp.bfloat16)
    send_rows = jnp.dot(placing, pair_rows, preferred_element_type=jnp.float32).astype(jnp.bfloat16)
    send_ids = jnp.full((groups * capacity,), -1, jnp.bfloat16).at[target].set(
        pair_edge.astype(jnp.bfloat16)
    )
    id_row = jnp.pad(send_ids.reshape(groups, 1, capacity), ((0, 0), (0, 0), (0, row_width - capacity)))
    send = jnp.concatenate([send_rows.reshape(groups, capacity, row_width), id_row], axis=1)
    edge_count = EDGE_DEV
    recv = lax.all_to_all(send, ("gx", "gy"), split_axis=0, concat_axis=0, tiled=True)
    flat_rows = recv[:, :capacity, :].reshape(groups * capacity, row_width)
    flat_ids = recv[:, capacity, :capacity].reshape(groups * capacity).astype(jnp.int32)
    edge_onehot = (lax.iota(jnp.int32, edge_count)[:, None] == flat_ids[None, :]).astype(
        jnp.bfloat16
    )
    edge_rows = jnp.dot(edge_onehot, flat_rows, preferred_element_type=jnp.float32).astype(
        jnp.bfloat16
    )
    first = jax.nn.silu(
        jnp.dot(edge_rows, mlp_in, preferred_element_type=jnp.float32) + mlp_in_bias
    ).astype(jnp.bfloat16)
    second = jax.nn.silu(
        jnp.dot(first, mlp_mid, preferred_element_type=jnp.float32) + mlp_mid_bias
    ).astype(jnp.bfloat16)
    edge_scores = jnp.dot(second, mlp_out, preferred_element_type=jnp.float32)
    owner_picks = flat_ids[:, None] == lax.iota(jnp.int32, edge_count)[None, :]
    owner_scores = jnp.sum(jnp.where(owner_picks, edge_scores[None, :], 0.0), axis=1)
    returned = lax.all_to_all(
        owner_scores.reshape(groups, capacity), ("gx", "gy"), split_axis=0, concat_axis=0, tiled=True
    ).reshape(groups * capacity)
    back_picks = target[:, None] == lax.iota(jnp.int32, groups * capacity)[None, :]
    return jnp.sum(jnp.where(back_picks, returned[None, :], 0.0), axis=1)


def solution(mesh):
    placed = (
        P(None, "gx", "gy", "gz"),
        P("gx", "gy", "gz"),
        P(),
        P(),
        P(("gx", "gy", "gz"), None),
        P(("gx", "gy", "gz")),
        P(),
        P(),
        P(),
        P(),
        P(),
    )
    return jax.shard_map(
        body, mesh=mesh, in_specs=placed, out_specs=P(("gx", "gy", "gz")), check_vma=False
    )
```

```python
import jax
import jax.numpy as jnp
from jax import lax
from jax.sharding import PartitionSpec as P

BINS = 8
EDGE_DEV = 64


def extended(cells, sides, width):
    for axis, dim in sides:
        count = lax.axis_size(axis)
        ends = count - 1
        head = lax.slice_in_dim(cells, 0, width, axis=dim)
        tail = lax.slice_in_dim(cells, cells.shape[dim] - width, cells.shape[dim], axis=dim)
        cells = jnp.concatenate(
            [
                lax.ppermute(tail, axis, [(i, (i + 1) % count) for i in range(ends)]),
                cells,
                lax.ppermute(head, axis, [((i + 1) % count, i) for i in range(ends)]),
            ],
            axis=dim,
        )
    return cells


def banded_weight(conv_weight, channels):
    taps = conv_weight.reshape(3, 3, 3, channels, channels).transpose(0, 1, 2, 4, 3)
    empty = jnp.zeros((3, 3, channels, channels), conv_weight.dtype)

    def block(part, zi, zo):
        shift = zi - zo if part == 1 else (-1 if (part, zi, zo) == (0, 3, 0) else None)
        if part == 2 and (zi, zo) == (0, 3):
            shift = 1
        if shift is None or abs(shift) > 1:
            return empty
        return taps[:, :, shift + 1]

    parts = [
        jnp.concatenate(
            [jnp.concatenate([block(part, zi, zo) for zo in range(4)], axis=3) for zi in range(4)],
            axis=2,
        )
        for part in range(3)
    ]
    return jnp.stack(parts, axis=2).reshape(27 * 4 * channels, 4 * channels)


def conv_lane_dense(padded, low, high, conv_weight, channels):
    px, py, nchunk, chunk = padded.shape
    weight = banded_weight(conv_weight, channels)
    blocks = weight.reshape(9, 3, chunk, chunk)
    empty = jnp.zeros((px, py, 1, chunk), padded.dtype)
    parts = (
        jnp.concatenate([empty, padded[:, :, :-1]], axis=2),
        padded,
        jnp.concatenate([padded[:, :, 1:], empty], axis=2),
    )
    trio = jnp.concatenate(parts, axis=3)
    grouped = weight.reshape(9, 3 * chunk, chunk)
    main = None
    for dx in range(3):
        for dy in range(3):
            term = jnp.dot(
                trio[dx : dx + px - 2, dy : dy + py - 2],
                grouped[dx * 3 + dy],
                preferred_element_type=jnp.float32,
            )
            main = term if main is None else main + term
    low_chunk = jnp.pad(low, ((0, 0), (0, 0), (chunk - channels, 0)))
    high_chunk = jnp.pad(high, ((0, 0), (0, 0), (0, chunk - channels)))

    def edge(halo, part):
        pieces = [halo[dx : dx + px - 2, dy : dy + py - 2] for dx in range(3) for dy in range(3)]
        return jnp.dot(
            jnp.concatenate(pieces, axis=2),
            blocks[:, part].reshape(9 * chunk, chunk),
            preferred_element_type=jnp.float32,
        )

    main = main.at[:, :, 0, :].add(edge(low_chunk, 0))
    return main.at[:, :, nchunk - 1, :].add(edge(high_chunk, 2))

def body(
    features,
    voxel_slot,
    conv_weight,
    conv_bias,
    pair_owner,
    pair_edge,
    mlp_in,
    mlp_in_bias,
    mlp_mid,
    mlp_mid_bias,
    mlp_out,
):
    channels, extent_x, extent_y, extent_z = features.shape
    volume = extent_x * extent_y * extent_z
    chunk = 4 * channels
    cells = (
        features.reshape(channels, extent_x, extent_y, extent_z // 4, 4)
        .transpose(1, 2, 3, 4, 0)
        .reshape(extent_x, extent_y, extent_z // 4, chunk)
    )
    padded = extended(cells, (("gx", 0), ("gy", 1)), 1)
    count_z = lax.axis_size("gz")
    low = lax.ppermute(
        padded[:, :, -1, chunk - channels :], "gz", [(i, i + 1) for i in range(count_z - 1)]
    )
    high = lax.ppermute(padded[:, :, 0, :channels], "gz", [(i + 1, i) for i in range(count_z - 1)])
    total = conv_lane_dense(padded, low, high, conv_weight, channels).reshape(volume, channels)
    fields = jnp.maximum(total + conv_bias[None, :], 0.0).astype(jnp.bfloat16)
    pair_count = pair_edge.shape[0]
    slot_count = pair_count * BINS
    slots_flat = voxel_slot.reshape(volume)
    onehot = (slots_flat[:, None] == lax.iota(jnp.int32, slot_count)[None, :]).astype(jnp.bfloat16)
    pooled = lax.dot_general(
        onehot, fields, (((0,), (0,)), ((), ())), preferred_element_type=jnp.float32
    ) * (slot_count / volume)
    row_width = BINS * channels
    pair_rows = (
        pooled.reshape(BINS, pair_count, channels)
        .transpose(1, 0, 2)
        .reshape(pair_count, row_width)
        .astype(jnp.bfloat16)
    )
    size_gx = lax.axis_size("gx")
    size_gy = lax.axis_size("gy")
    groups = size_gx * size_gy
    capacity = max(2, (5 * pair_count + 2 * groups - 1) // (2 * groups))
    capacity = max(capacity, 7)
    owners = pair_owner[:, 0]
    owner_marks = (owners[:, None] == lax.iota(jnp.int32, groups)[None, :]).astype(jnp.int32)
    earlier = jnp.cumsum(owner_marks, axis=0) - owner_marks
    slot_rank = jnp.sum(earlier * owner_marks, axis=1)
    target = owners * capacity + slot_rank
    placing = (lax.iota(jnp.int32, groups * capacity)[:, None] == target[None, :]).astype(jnp.bfloat16)
    send_rows = jnp.dot(placing, pair_rows, preferred_element_type=jnp.float32).astype(jnp.bfloat16)
    send_ids = jnp.full((groups * capacity,), -1, jnp.bfloat16).at[target].set(
        pair_edge.astype(jnp.bfloat16)
    )
    id_row = jnp.pad(send_ids.reshape(groups, 1, capacity), ((0, 0), (0, 0), (0, row_width - capacity)))
    send = jnp.concatenate([send_rows.reshape(groups, capacity, row_width), id_row], axis=1)
    edge_count = EDGE_DEV
    recv = lax.all_to_all(send, ("gx", "gy"), split_axis=0, concat_axis=0, tiled=True)
    flat_rows = recv[:, :capacity, :].reshape(groups * capacity, row_width)
    flat_ids = recv[:, capacity, :capacity].reshape(groups * capacity).astype(jnp.int32)
    edge_onehot = (lax.iota(jnp.int32, edge_count)[:, None] == flat_ids[None, :]).astype(
        jnp.bfloat16
    )
    edge_rows = jnp.dot(edge_onehot, flat_rows, preferred_element_type=jnp.float32).astype(
        jnp.bfloat16
    )
    first = jax.nn.silu(
        jnp.dot(edge_rows, mlp_in, preferred_element_type=jnp.float32) + mlp_in_bias
    ).astype(jnp.bfloat16)
    second = jax.nn.silu(
        jnp.dot(first, mlp_mid, preferred_element_type=jnp.float32) + mlp_mid_bias
    ).astype(jnp.bfloat16)
    edge_scores = jnp.dot(second, mlp_out, preferred_element_type=jnp.float32)
    owner_picks = flat_ids[:, None] == lax.iota(jnp.int32, edge_count)[None, :]
    owner_scores = jnp.sum(jnp.where(owner_picks, edge_scores[None, :], 0.0), axis=1)
    returned = lax.all_to_all(
        owner_scores.reshape(groups, capacity), ("gx", "gy"), split_axis=0, concat_axis=0, tiled=True
    ).reshape(groups * capacity)
    back_picks = target[:, None] == lax.iota(jnp.int32, groups * capacity)[None, :]
    return jnp.sum(jnp.where(back_picks, returned[None, :], 0.0), axis=1)


def solution(mesh):
    placed = (
        P(None, "gx", "gy", "gz"),
        P("gx", "gy", "gz"),
        P(),
        P(),
        P(("gx", "gy", "gz"), None),
        P(("gx", "gy", "gz")),
        P(),
        P(),
        P(),
        P(),
        P(),
    )
    return jax.shard_map(
        body, mesh=mesh, in_specs=placed, out_specs=P(("gx", "gy", "gz")), check_vma=False
    )
```

```python
import jax
import jax.numpy as jnp
from jax import lax
from jax.sharding import PartitionSpec as P

BINS = 8
EDGE_DEV = 64


def extended(cells, sides, width):
    for axis, dim in sides:
        count = lax.axis_size(axis)
        ends = count - 1
        head = lax.slice_in_dim(cells, 0, width, axis=dim)
        tail = lax.slice_in_dim(cells, cells.shape[dim] - width, cells.shape[dim], axis=dim)
        cells = jnp.concatenate(
            [
                lax.ppermute(tail, axis, [(i, (i + 1) % count) for i in range(ends)]),
                cells,
                lax.ppermute(head, axis, [((i + 1) % count, i) for i in range(ends)]),
            ],
            axis=dim,
        )
    return cells


def banded_weight(conv_weight, channels):
    taps = conv_weight.reshape(3, 3, 3, channels, channels).transpose(0, 1, 2, 4, 3)
    empty = jnp.zeros((3, 3, channels, channels), conv_weight.dtype)

    def block(part, zi, zo):
        shift = zi - zo if part == 1 else (-1 if (part, zi, zo) == (0, 3, 0) else None)
        if part == 2 and (zi, zo) == (0, 3):
            shift = 1
        if shift is None or abs(shift) > 1:
            return empty
        return taps[:, :, shift + 1]

    parts = [
        jnp.concatenate(
            [jnp.concatenate([block(part, zi, zo) for zo in range(4)], axis=3) for zi in range(4)],
            axis=2,
        )
        for part in range(3)
    ]
    return jnp.stack(parts, axis=2).reshape(27 * 4 * channels, 4 * channels)


def conv_lane_dense(padded, low, high, conv_weight, channels):
    px, py, nchunk, chunk = padded.shape
    weight = banded_weight(conv_weight, channels)
    blocks = weight.reshape(9, 3, chunk, chunk)
    empty = jnp.zeros((px, py, 1, chunk), padded.dtype)
    parts = (
        jnp.concatenate([empty, padded[:, :, :-1]], axis=2),
        padded,
        jnp.concatenate([padded[:, :, 1:], empty], axis=2),
    )
    slabs = [
        parts[p][dx : dx + px - 2, dy : dy + py - 2]
        for dx in range(3)
        for dy in range(3)
        for p in range(3)
    ]
    main = jnp.dot(jnp.concatenate(slabs, axis=3), weight, preferred_element_type=jnp.float32)
    low_chunk = jnp.pad(low, ((0, 0), (0, 0), (chunk - channels, 0)))
    high_chunk = jnp.pad(high, ((0, 0), (0, 0), (0, chunk - channels)))

    def edge(halo, part):
        pieces = [halo[dx : dx + px - 2, dy : dy + py - 2] for dx in range(3) for dy in range(3)]
        return jnp.dot(
            jnp.concatenate(pieces, axis=2),
            blocks[:, part].reshape(9 * chunk, chunk),
            preferred_element_type=jnp.float32,
        )

    main = main.at[:, :, 0, :].add(edge(low_chunk, 0))
    return main.at[:, :, nchunk - 1, :].add(edge(high_chunk, 2))

def body(
    features,
    voxel_slot,
    conv_weight,
    conv_bias,
    pair_owner,
    pair_edge,
    mlp_in,
    mlp_in_bias,
    mlp_mid,
    mlp_mid_bias,
    mlp_out,
):
    channels, extent_x, extent_y, extent_z = features.shape
    volume = extent_x * extent_y * extent_z
    chunk = 4 * channels

    def lane_dense(block):
        return (
            block.reshape(channels, block.shape[1], extent_y, extent_z // 4, 4)
            .transpose(1, 2, 3, 4, 0)
            .reshape(block.shape[1], extent_y, extent_z // 4, chunk)
        )

    count_x = lax.axis_size("gx")
    from_below = lax.ppermute(features[:, -1:], "gx", [(i, i + 1) for i in range(count_x - 1)])
    from_above = lax.ppermute(features[:, :1], "gx", [(i + 1, i) for i in range(count_x - 1)])
    cells = jnp.concatenate(
        [lane_dense(from_below), lane_dense(features), lane_dense(from_above)], axis=0
    )
    padded = extended(cells, (("gy", 1),), 1)
    count_z = lax.axis_size("gz")
    low = lax.ppermute(
        padded[:, :, -1, chunk - channels :], "gz", [(i, i + 1) for i in range(count_z - 1)]
    )
    high = lax.ppermute(padded[:, :, 0, :channels], "gz", [(i + 1, i) for i in range(count_z - 1)])
    total = conv_lane_dense(padded, low, high, conv_weight, channels).reshape(volume, channels)
    fields = jnp.maximum(total + conv_bias[None, :], 0.0).astype(jnp.bfloat16)
    pair_count = pair_edge.shape[0]
    slot_count = pair_count * BINS
    slots_flat = voxel_slot.reshape(volume)
    onehot = (slots_flat[:, None] == lax.iota(jnp.int32, slot_count)[None, :]).astype(jnp.bfloat16)
    pooled = lax.dot_general(
        onehot, fields, (((0,), (0,)), ((), ())), preferred_element_type=jnp.float32
    ) * (slot_count / volume)
    row_width = BINS * channels
    pair_rows = (
        pooled.reshape(BINS, pair_count, channels)
        .transpose(1, 0, 2)
        .reshape(pair_count, row_width)
        .astype(jnp.bfloat16)
    )
    size_gx = lax.axis_size("gx")
    size_gy = lax.axis_size("gy")
    groups = size_gx * size_gy
    capacity = max(2, (5 * pair_count + 2 * groups - 1) // (2 * groups))
    capacity = max(capacity, 7)
    owners = pair_owner[:, 0]
    owner_marks = (owners[:, None] == lax.iota(jnp.int32, groups)[None, :]).astype(jnp.int32)
    earlier = jnp.cumsum(owner_marks, axis=0) - owner_marks
    slot_rank = jnp.sum(earlier * owner_marks, axis=1)
    target = owners * capacity + slot_rank
    placing = (lax.iota(jnp.int32, groups * capacity)[:, None] == target[None, :]).astype(jnp.bfloat16)
    send_rows = jnp.dot(placing, pair_rows, preferred_element_type=jnp.float32).astype(jnp.bfloat16)
    send_ids = jnp.full((groups * capacity,), -1, jnp.bfloat16).at[target].set(
        pair_edge.astype(jnp.bfloat16)
    )
    id_row = jnp.pad(send_ids.reshape(groups, 1, capacity), ((0, 0), (0, 0), (0, row_width - capacity)))
    send = jnp.concatenate([send_rows.reshape(groups, capacity, row_width), id_row], axis=1)
    edge_count = EDGE_DEV
    recv = lax.all_to_all(send, ("gx", "gy"), split_axis=0, concat_axis=0, tiled=True)
    flat_rows = recv[:, :capacity, :].reshape(groups * capacity, row_width)
    flat_ids = recv[:, capacity, :capacity].reshape(groups * capacity).astype(jnp.int32)
    edge_onehot = (lax.iota(jnp.int32, edge_count)[:, None] == flat_ids[None, :]).astype(
        jnp.bfloat16
    )
    edge_rows = jnp.dot(edge_onehot, flat_rows, preferred_element_type=jnp.float32).astype(
        jnp.bfloat16
    )
    first = jax.nn.silu(
        jnp.dot(edge_rows, mlp_in, preferred_element_type=jnp.float32) + mlp_in_bias
    ).astype(jnp.bfloat16)
    second = jax.nn.silu(
        jnp.dot(first, mlp_mid, preferred_element_type=jnp.float32) + mlp_mid_bias
    ).astype(jnp.bfloat16)
    edge_scores = jnp.dot(second, mlp_out, preferred_element_type=jnp.float32)
    owner_picks = flat_ids[:, None] == lax.iota(jnp.int32, edge_count)[None, :]
    owner_scores = jnp.sum(jnp.where(owner_picks, edge_scores[None, :], 0.0), axis=1)
    returned = lax.all_to_all(
        owner_scores.reshape(groups, capacity), ("gx", "gy"), split_axis=0, concat_axis=0, tiled=True
    ).reshape(groups * capacity)
    back_picks = target[:, None] == lax.iota(jnp.int32, groups * capacity)[None, :]
    return jnp.sum(jnp.where(back_picks, returned[None, :], 0.0), axis=1)


def solution(mesh):
    placed = (
        P(None, "gx", "gy", "gz"),
        P("gx", "gy", "gz"),
        P(),
        P(),
        P(("gx", "gy", "gz"), None),
        P(("gx", "gy", "gz")),
        P(),
        P(),
        P(),
        P(),
        P(),
    )
    return jax.shard_map(
        body, mesh=mesh, in_specs=placed, out_specs=P(("gx", "gy", "gz")), check_vma=False
    )
```
